32 devices in a mesh: space: 8 (over z, y), filt: 4 (over x, core).
Axes of the slice: x: 2, y: 2, z: 4, core: 2. Of those that a mesh axis runs over, the one named last changes fastest.
Arguments:
- inputs: bfloat16 [16, 32, 32, 512], P('space', None, None, 'filt'), may hold values from -6 to 6
- grad_out: bfloat16 [16, 32, 32, 512], P('space', None, None, 'filt'), may hold values from -6 to 6
- weights: bfloat16 [3, 3, 3, 512, 512], P(None, None, None, None, 'filt'), may hold values from -0.0546875 to 0.0546875
Outputs:
- grad_inputs: bfloat16 [16, 32, 32, 512], P('space', None, None, 'filt')
- weight_grad: float32 [3, 3, 3, 512, 512], P(None, None, None, None, 'filt')
The draws below stay inside these ranges and needn't reach their ends.
All inputs are finite; a program needn't handle non-finite values.
Results may differ from the reference program's by a relative error of at most 0.001.
Values may be sent and summed in bfloat16 or wider, within the bound.
No kernel may reach another device: no remote copies, remote signals or barrier semaphores. Data moves between devices by JAX's collectives and lax.ppermute only.
A program may use at most 128 MiB of HBM per device.

```python
import math
import jax
import jax.numpy as jnp

CIN = 512
COUT = 512
NY = 32
NZ = 32
NX = 16


def shard_levels(key, dims, split, low, high):
    def one(axis_at, parts):
        steps = jax.random.uniform(jax.random.fold_in(jax.random.fold_in(key, 6), axis_at), (parts,), jnp.float32, low / len(split), high / len(split))
        return jnp.repeat(jnp.exp(steps), dims[axis_at] // parts).reshape((-1,) + (1,) * (len(dims) - axis_at - 1))

    gain = one(*split[0])
    for cut in split[1:]:
        gain = gain * one(*cut)
    return gain


def bell_draw(stream_key, shape, spread, reach, split=(), kind=jnp.bfloat16):
    values = jax.random.normal(stream_key, shape, jnp.float32) * spread
    if len(split) > 0:
        values = shard_levels(stream_key, shape, split, -0.22, 0.18) * values
    return jnp.clip(values, min=-reach, max=reach).astype(kind)


def setup_inputs(seed: int = 0) -> dict:
    keys = jax.random.split(jax.random.key(seed), 4)
    inputs = bell_draw(keys[0], (NX, NY, NZ, CIN), 1.0, 6.0, ((0, 8), (3, 4)))
    grad_out = bell_draw(keys[1], (NX, NY, NZ, COUT), 1.0, 6.0, ((0, 8), (3, 4)))
    weights = bell_draw(keys[2], (3, 3, 3, CIN, COUT), (27 * CIN) ** -0.5, 0.0546875, ((4, 4),))
    return dict(inputs=inputs, grad_out=grad_out, weights=weights)


def reference(inputs, grad_out, weights):
    nx, ny, nz, cin = inputs.shape
    cout = grad_out.shape[3]
    voxels = nx * ny * nz
    padded_in = jnp.pad(inputs, ((1, 1), (1, 1), (1, 1), (0, 0)))
    padded_grad = jnp.pad(grad_out, ((1, 1), (1, 1), (1, 1), (0, 0)))
    grad_flat = grad_out.reshape(voxels, cout)
    tap_list = []
    data_term = jnp.zeros((voxels, cin), jnp.float32)
    for a in range(3):
        for b in range(3):
            for c in range(3):
                shifted = padded_in[a:a + nx, b:b + ny, c:c + nz, :].reshape(voxels, cin)
                tap_list.append(jnp.dot(shifted.T, grad_flat, preferred_element_type=jnp.float32))
                moved = padded_grad[2 - a:2 - a + nx, 2 - b:2 - b + ny, 2 - c:2 - c + nz, :].reshape(voxels, cout)
                data_term = data_term + jnp.dot(moved, weights[a, b, c].T, preferred_element_type=jnp.float32)
    weight_grad = jnp.stack(tap_list).reshape(3, 3, 3, cin, cout) * (1.0 / math.sqrt(voxels))
    grad_inputs = data_term.reshape(nx, ny, nz, cin).astype(jnp.bfloat16)
    return (grad_inputs, weight_grad)
```

```python
import math

import jax
import jax.numpy as jnp
import numpy as np
from jax import lax
from jax.sharding import PartitionSpec as P


def extended(array, sides, width):
    for axis, dim in sides:
        size, length = (lax.axis_size(axis), array.shape[dim])
        up = [(i, (i + 1) % size) for i in range(size - 1)]
        down = [(j, i) for i, j in up]
        last = lax.slice_in_dim(array, length - width, length, axis=dim)
        first = lax.slice_in_dim(array, 0, width, axis=dim)
        before = lax.ppermute(last, axis, up)
        after = lax.ppermute(first, axis, down)
        array = jnp.concatenate([before, array, after], axis=dim)
    return array


def ring_order(n):
    if n % 2:
        return list(range(n))
    return list(range(0, n, 2)) + list(range(n - 1, 0, -2))


def ring_sum_dir(x, axis, order, base, chunk, scale):
    n = len(order)
    pos_tab = np.zeros(n, np.int32)
    for i, s in enumerate(order):
        pos_tab[s] = i
    p = jnp.asarray(pos_tab)[lax.axis_index(axis)]
    perm = [(order[i], order[(i + 1) % n]) for i in range(n)]

    def piece(k):
        start = base + ((p - k) % n) * chunk
        return lax.dynamic_slice_in_dim(x, start, chunk, axis=1)

    acc = piece(0)
    for k in range(n - 1):
        acc = lax.ppermute(acc, axis, perm) + piece(k + 1)
    acc = acc * scale
    out = jnp.zeros(x.shape[:1] + (n * chunk,) + x.shape[2:], x.dtype)
    out = lax.dynamic_update_slice_in_dim(out, acc, ((p + 1) % n) * chunk, axis=1)
    cur = acc
    for k in range(n - 1):
        cur = lax.ppermute(cur, axis, perm)
        out = lax.dynamic_update_slice_in_dim(out, cur, ((p - k) % n) * chunk, axis=1)
    return out


def ring_sum(x, axis, scale):
    n = lax.axis_size(axis)
    rows = x.shape[1]
    if n == 1:
        return x * scale
    if rows % (2 * n):
        return lax.psum(x, axis) * scale
    order = ring_order(n)
    chunk = rows // (2 * n)
    half = rows // 2
    first = ring_sum_dir(x, axis, order, 0, chunk, scale)
    second = ring_sum_dir(x, axis, order[::-1], half, chunk, scale)
    return jnp.concatenate([first, second], axis=1)


def shards(inputs, grad_out, weights):
    planes, ny, nz, fshare = grad_out.shape
    cin = weights.shape[3]
    voxels = planes * ny * nz
    scale = 1.0 / math.sqrt(voxels * lax.axis_size("space"))
    grad_rimmed = extended(grad_out, (("space", 0),), 1)
    grad_padded = jnp.pad(grad_rimmed, ((0, 0), (1, 1), (1, 1), (0, 0)))
    grad_flat = grad_out.reshape(voxels, fshare)
    gathered = lax.all_gather(inputs, "filt", axis=3, tiled=True)
    wide_rimmed = extended(gathered, (("space", 0),), 1)
    width = wide_rimmed.shape[3]
    padded = jnp.pad(wide_rimmed, ((0, 0), (1, 1), (1, 1), (0, 0)))
    rows_list = []
    for tap_a in range(3):
        for b in range(3):
            for c in range(3):
                shifted = padded[tap_a : tap_a + planes, b : b + ny, c : c + nz, :].reshape(
                    voxels, width
                )
                rows_list.append(
                    lax.dot_general(
                        shifted,
                        grad_flat,
                        (((0,), (0,)), ((), ())),
                        preferred_element_type=jnp.float32,
                    )
                )
    tap_sums = jnp.stack(rows_list)
    weight_grad = ring_sum(tap_sums, "space", scale).reshape(3, 3, 3, width, fshare)
    data_term = jnp.zeros((voxels, cin), jnp.float32)
    for a in range(3):
        moved_list = []
        for data_b in range(3):
            for data_c in range(3):
                moved_list.append(
                    grad_padded[
                        2 - a : 2 - a + planes,
                        2 - data_b : 2 - data_b + ny,
                        2 - data_c : 2 - data_c + nz,
                        :,
                    ].reshape(voxels, fshare)
                )
        stacked = jnp.stack(moved_list, axis=1).reshape(voxels, 3, 3, fshare)
        data_term = data_term + lax.dot_general(
            stacked,
            weights[a],
            (((1, 2, 3), (0, 1, 3)), ((), ())),
            preferred_element_type=jnp.float32,
        )
    grad_inputs = lax.psum_scatter(
        data_term.reshape(planes, ny, nz, cin), "filt", scatter_dimension=3, tiled=True
    ).astype(jnp.bfloat16)
    return (grad_inputs, weight_grad)


def solution(mesh):
    placed = (
        P("space", None, None, "filt"),
        P("space", None, None, "filt"),
        P(None, None, None, None, "filt"),
    )
    return jax.shard_map(
        shards,
        mesh=mesh,
        in_specs=placed,
        out_specs=(P("space", None, None, "filt"), P(None, None, None, None, "filt")),
        check_vma=False,
    )
```

```python
import math

import jax
import jax.numpy as jnp
import numpy as np
from jax import lax
from jax.sharding import PartitionSpec as P


def extended(array, sides, width):
    for axis, dim in sides:
        size, length = (lax.axis_size(axis), array.shape[dim])
        up = [(i, (i + 1) % size) for i in range(size - 1)]
        down = [(j, i) for i, j in up]
        last = lax.slice_in_dim(array, length - width, length, axis=dim)
        first = lax.slice_in_dim(array, 0, width, axis=dim)
        before = lax.ppermute(last, axis, up)
        after = lax.ppermute(first, axis, down)
        array = jnp.concatenate([before, array, after], axis=dim)
    return array


def ring_order(n):
    if n % 2:
        return list(range(n))
    return list(range(0, n, 2)) + list(range(n - 1, 0, -2))


def ring_sum_dir(x, axis, order, base, chunk, scale):
    n = len(order)
    pos_tab = np.zeros(n, np.int32)
    for i, s in enumerate(order):
        pos_tab[s] = i
    p = jnp.asarray(pos_tab)[lax.axis_index(axis)]
    perm = [(order[i], order[(i + 1) % n]) for i in range(n)]

    def piece(k):
        start = base + ((p - k) % n) * chunk
        return lax.dynamic_slice_in_dim(x, start, chunk, axis=1)

    acc = piece(0)
    for k in range(n - 1):
        acc = lax.ppermute(acc, axis, perm) + piece(k + 1)
    acc = acc * scale
    out = jnp.zeros(x.shape[:1] + (n * chunk,) + x.shape[2:], x.dtype)
    out = lax.dynamic_update_slice_in_dim(out, acc, ((p + 1) % n) * chunk, axis=1)
    cur = acc
    for k in range(n - 1):
        cur = lax.ppermute(cur, axis, perm)
        out = lax.dynamic_update_slice_in_dim(out, cur, ((p - k) % n) * chunk, axis=1)
    return out


def ring_sum(x, axis, scale):
    n = lax.axis_size(axis)
    rows = x.shape[1]
    if n == 1:
        return x * scale
    if rows % (2 * n):
        return lax.psum(x, axis) * scale
    order = ring_order(n)
    chunk = rows // (2 * n)
    half = rows // 2
    first = ring_sum_dir(x, axis, order, 0, chunk, scale)
    second = ring_sum_dir(x, axis, order[::-1], half, chunk, scale)
    return jnp.concatenate([first, second], axis=1)


def shards(inputs, grad_out, weights):
    planes, ny, nz, fshare = grad_out.shape
    cin = weights.shape[3]
    voxels = planes * ny * nz
    scale = 1.0 / math.sqrt(voxels * lax.axis_size("space"))
    grad_rimmed = extended(grad_out, (("space", 0),), 1)
    grad_padded = jnp.pad(grad_rimmed, ((0, 0), (1, 1), (1, 1), (0, 0)))
    gathered = lax.all_gather(inputs, "filt", axis=3, tiled=True)
    width = gathered.shape[3]
    in_flat = gathered.reshape(voxels, width)
    rows_list = []
    for tap_a in range(3):
        for b in range(3):
            for c in range(3):
                moved = grad_padded[
                    2 - tap_a : 2 - tap_a + planes, 2 - b : 2 - b + ny, 2 - c : 2 - c + nz, :
                ].reshape(voxels, fshare)
                rows_list.append(
                    lax.dot_general(
                        in_flat,
                        moved,
                        (((0,), (0,)), ((), ())),
                        preferred_element_type=jnp.float32,
                    )
                )
    tap_sums = jnp.stack(rows_list)
    tap_sums, grad_padded, weights = lax.optimization_barrier((tap_sums, grad_padded, weights))
    weight_grad = ring_sum(tap_sums, "space", scale).reshape(3, 3, 3, width, fshare)
    data_term = jnp.zeros((voxels, cin), jnp.float32)
    for a in range(3):
        moved_list = []
        for data_b in range(3):
            for data_c in range(3):
                moved_list.append(
                    grad_padded[
                        2 - a : 2 - a + planes,
                        2 - data_b : 2 - data_b + ny,
                        2 - data_c : 2 - data_c + nz,
                        :,
                    ].reshape(voxels, fshare)
                )
        stacked = jnp.stack(moved_list, axis=1).reshape(voxels, 3, 3, fshare)
        data_term = data_term + lax.dot_general(
            stacked,
            weights[a],
            (((1, 2, 3), (0, 1, 3)), ((), ())),
            preferred_element_type=jnp.float32,
        )
    grad_inputs = lax.psum_scatter(
        data_term.reshape(planes, ny, nz, cin), "filt", scatter_dimension=3, tiled=True
    ).astype(jnp.bfloat16)
    return (grad_inputs, weight_grad)


def solution(mesh):
    placed = (
        P("space", None, None, "filt"),
        P("space", None, None, "filt"),
        P(None, None, None, None, "filt"),
    )
    return jax.shard_map(
        shards,
        mesh=mesh,
        in_specs=placed,
        out_specs=(P("space", None, None, "filt"), P(None, None, None, None, "filt")),
        check_vma=False,
    )
```

```python
import math

import jax
import jax.numpy as jnp
import numpy as np
from jax import lax
from jax.sharding import PartitionSpec as P


def extended(array, sides, width):
    for axis, dim in sides:
        size, length = (lax.axis_size(axis), array.shape[dim])
        up = [(i, (i + 1) % size) for i in range(size - 1)]
        down = [(j, i) for i, j in up]
        last = lax.slice_in_dim(array, length - width, length, axis=dim)
        first = lax.slice_in_dim(array, 0, width, axis=dim)
        before = lax.ppermute(last, axis, up)
        after = lax.ppermute(first, axis, down)
        array = jnp.concatenate([before, array, after], axis=dim)
    return array


def ring_order(n):
    if n % 2:
        return list(range(n))
    return list(range(0, n, 2)) + list(range(n - 1, 0, -2))


def ring_sum_dir(x, axis, order, base, chunk, scale, taps):
    n = len(order)
    pos_tab = np.zeros(n, np.int32)
    for i, s in enumerate(order):
        pos_tab[s] = i
    p = jnp.asarray(pos_tab)[lax.axis_index(axis)]
    perm = [(order[i], order[(i + 1) % n]) for i in range(n)]

    def piece(k):
        start = base + ((p - k) % n) * chunk
        return lax.dynamic_slice_in_dim(x, start, chunk, axis=0)

    acc = piece(0)
    for k in range(n - 1):
        acc = lax.ppermute(acc, axis, perm) + piece(k + 1)
    acc = acc * scale
    cout = x.shape[1] // taps
    out = jnp.zeros((taps, n * chunk, cout), x.dtype)

    def put(out, block, k):
        block = block.reshape(chunk, taps, cout).transpose(1, 0, 2)
        return lax.dynamic_update_slice_in_dim(out, block, (k % n) * chunk, axis=1)

    out = put(out, acc, p + 1)
    cur = acc
    for k in range(n - 1):
        cur = lax.ppermute(cur, axis, perm)
        out = put(out, cur, p - k)
    return out


def ring_sum(x, axis, scale):
    n = lax.axis_size(axis)
    rows, taps = x.shape[:2]
    if n == 1 or rows % (16 * n):
        return (lax.psum(x, axis) * scale).transpose(1, 0, 2)
    x = x.reshape(rows, -1)
    order = ring_order(n)
    chunk = rows // (2 * n)
    half = rows // 2
    first = ring_sum_dir(x, axis, order, 0, chunk, scale, taps)
    second = ring_sum_dir(x, axis, order[::-1], half, chunk, scale, taps)
    return jnp.concatenate([first, second], axis=1)


def shards(inputs, grad_out, weights):
    planes, ny, nz, fshare = grad_out.shape
    cin = weights.shape[3]
    voxels = planes * ny * nz
    scale = 1.0 / math.sqrt(voxels * lax.axis_size("space"))
    grad_rimmed = extended(grad_out, (("space", 0),), 1)
    grad_padded = jnp.pad(grad_rimmed, ((0, 0), (1, 1), (1, 1), (0, 0)))
    gathered = lax.all_gather(inputs, "filt", axis=3, tiled=True)
    width = gathered.shape[3]
    in_flat = gathered.reshape(voxels, width)
    stacks = []
    for a in range(3):
        moved_list = []
        for b in range(3):
            for c in range(3):
                moved_list.append(
                    grad_padded[
                        2 - a : 2 - a + planes, 2 - b : 2 - b + ny, 2 - c : 2 - c + nz, :
                    ].reshape(voxels, fshare)
                )
        stacks.append(jnp.stack(moved_list, axis=1))
    tap_rows = jnp.concatenate(
        [
            lax.dot_general(
                in_flat, st, (((0,), (0,)), ((), ())), preferred_element_type=jnp.float32
            )
            for st in stacks
        ],
        axis=1,
    )
    tap_rows, stacks, weights = lax.optimization_barrier((tap_rows, stacks, weights))
    weight_grad = ring_sum(tap_rows, "space", scale).reshape(3, 3, 3, width, fshare)
    data_term = jnp.zeros((voxels, cin), jnp.float32)
    for a in range(3):
        data_term = data_term + lax.dot_general(
            stacks[a].reshape(voxels, 3, 3, fshare),
            weights[a],
            (((1, 2, 3), (0, 1, 3)), ((), ())),
            preferred_element_type=jnp.float32,
        )
    grad_inputs = lax.psum_scatter(
        data_term.reshape(planes, ny, nz, cin), "filt", scatter_dimension=3, tiled=True
    ).astype(jnp.bfloat16)
    return (grad_inputs, weight_grad)


def solution(mesh):
    placed = (
        P("space", None, None, "filt"),
        P("space", None, None, "filt"),
        P(None, None, None, None, "filt"),
    )
    return jax.shard_map(
        shards,
        mesh=mesh,
        in_specs=placed,
        out_specs=(P("space", None, None, "filt"), P(None, None, None, None, "filt")),
        check_vma=False,
    )
```

```python
import math

import jax
import jax.numpy as jnp
import numpy as np
from jax import lax
from jax.sharding import PartitionSpec as P


def extended(array, sides, width):
    for axis, dim in sides:
        size, length = (lax.axis_size(axis), array.shape[dim])
        up = [(i, (i + 1) % size) for i in range(size - 1)]
        down = [(j, i) for i, j in up]
        last = lax.slice_in_dim(array, length - width, length, axis=dim)
        first = lax.slice_in_dim(array, 0, width, axis=dim)
        before = lax.ppermute(last, axis, up)
        after = lax.ppermute(first, axis, down)
        array = jnp.concatenate([before, array, after], axis=dim)
    return array


def ring_order(n):
    if n % 2:
        return list(range(n))
    return list(range(0, n, 2)) + list(range(n - 1, 0, -2))


def ring_sum(x, axis, scale, hold, parts=2):
    n = lax.axis_size(axis)
    rows = x.shape[1]
    rings = 2 * parts
    if n == 1 or rows % (8 * rings * n):
        return lax.psum(x, axis) * scale, hold
    chunk = rows // (rings * n)
    order = ring_order(n)
    plans = []
    for r in range(rings):
        ring = order if r % 2 == 0 else order[::-1]
        pos_tab = np.zeros(n, np.int32)
        for i, dev in enumerate(ring):
            pos_tab[dev] = i
        p = jnp.asarray(pos_tab)[lax.axis_index(axis)]
        perm = [(ring[i], ring[(i + 1) % n]) for i in range(n)]
        plans.append((r * n * chunk, p, perm))

    def piece(plan, k):
        base, p, _ = plan
        return lax.dynamic_slice_in_dim(x, base + ((p - k) % n) * chunk, chunk, axis=1)

    accs = [piece(plan, 0) for plan in plans]
    for k in range(n - 1):
        accs = [lax.ppermute(acc, axis, plan[2]) for acc, plan in zip(accs, plans)]
        if k == 0:
            accs, hold = lax.optimization_barrier((accs, hold))
        accs = [acc + piece(plan, k + 1) for acc, plan in zip(accs, plans)]
    accs = [acc * scale for acc in accs]
    outs = []
    for acc, (_, p, perm) in zip(accs, plans):
        out = jnp.zeros(x.shape[:1] + (n * chunk,) + x.shape[2:], x.dtype)
        outs.append(lax.dynamic_update_slice_in_dim(out, acc, ((p + 1) % n) * chunk, axis=1))
    curs = accs
    for k in range(n - 1):
        curs = [lax.ppermute(cur, axis, plan[2]) for cur, plan in zip(curs, plans)]
        outs = [
            lax.dynamic_update_slice_in_dim(out, cur, ((plan[1] - k) % n) * chunk, axis=1)
            for out, cur, plan in zip(outs, curs, plans)
        ]
    return jnp.concatenate(outs, axis=1), hold


def shards(inputs, grad_out, weights):
    planes, ny, nz, fshare = grad_out.shape
    cin = weights.shape[3]
    voxels = planes * ny * nz
    scale = 1.0 / math.sqrt(voxels * lax.axis_size("space"))
    grad_rimmed = extended(grad_out, (("space", 0),), 1)
    grad_padded = jnp.pad(grad_rimmed, ((0, 0), (1, 1), (1, 1), (0, 0)))
    gathered = lax.all_gather(inputs, "filt", axis=3, tiled=True)
    width = gathered.shape[3]
    in_flat = gathered.reshape(voxels, width)
    rows_list = []
    for tap_a in range(3):
        for b in range(3):
            for c in range(3):
                moved = grad_padded[
                    2 - tap_a : 2 - tap_a + planes, 2 - b : 2 - b + ny, 2 - c : 2 - c + nz, :
                ].reshape(voxels, fshare)
                rows_list.append(
                    lax.dot_general(
                        in_flat,
                        moved,
                        (((0,), (0,)), ((), ())),
                        preferred_element_type=jnp.float32,
                    )
                )
    tap_sums = jnp.stack(rows_list)
    summed, (grad_padded, weights) = ring_sum(tap_sums, "space", scale, (grad_padded, weights))
    weight_grad = summed.reshape(3, 3, 3, width, fshare)
    data_term = jnp.zeros((voxels, cin), jnp.float32)
    for a in range(3):
        moved_list = []
        for data_b in range(3):
            for data_c in range(3):
                moved_list.append(
                    grad_padded[
                        2 - a : 2 - a + planes,
                        2 - data_b : 2 - data_b + ny,
                        2 - data_c : 2 - data_c + nz,
                        :,
                    ].reshape(voxels, fshare)
                )
        stacked = jnp.stack(moved_list, axis=1).reshape(voxels, 3, 3, fshare)
        data_term = data_term + lax.dot_general(
            stacked,
            weights[a],
            (((1, 2, 3), (0, 1, 3)), ((), ())),
            preferred_element_type=jnp.float32,
        )
    grad_inputs = lax.psum_scatter(
        data_term.reshape(planes, ny, nz, cin), "filt", scatter_dimension=3, tiled=True
    ).astype(jnp.bfloat16)
    return (grad_inputs, weight_grad)


def solution(mesh):
    placed = (
        P("space", None, None, "filt"),
        P("space", None, None, "filt"),
        P(None, None, None, None, "filt"),
    )
    return jax.shard_map(
        shards,
        mesh=mesh,
        in_specs=placed,
        out_specs=(P("space", None, None, "filt"), P(None, None, None, None, "filt")),
        check_vma=False,
    )
```

```python
import math

import jax
import jax.numpy as jnp
import numpy as np
from jax import lax
from jax.sharding import PartitionSpec as P


def extended(array, sides, width):
    for axis, dim in sides:
        size, length = (lax.axis_size(axis), array.shape[dim])
        up = [(i, (i + 1) % size) for i in range(size - 1)]
        down = [(j, i) for i, j in up]
        last = lax.slice_in_dim(array, length - width, length, axis=dim)
        first = lax.slice_in_dim(array, 0, width, axis=dim)
        before = lax.ppermute(last, axis, up)
        after = lax.ppermute(first, axis, down)
        array = jnp.concatenate([before, array, after], axis=dim)
    return array


def ring_order(n):
    if n % 2:
        return list(range(n))
    return list(range(0, n, 2)) + list(range(n - 1, 0, -2))


def ring_sum(x, axis, scale, hold, parts=1):
    n = lax.axis_size(axis)
    rows = x.shape[1]
    rings = 2 * parts
    if n == 1 or rows % (8 * rings * n):
        return lax.psum(x, axis) * scale, hold
    chunk = rows // (rings * n)
    order = ring_order(n)
    plans = []
    for r in range(rings):
        ring = order if r % 2 == 0 else order[::-1]
        pos_tab = np.zeros(n, np.int32)
        for i, dev in enumerate(ring):
            pos_tab[dev] = i
        p = jnp.asarray(pos_tab)[lax.axis_index(axis)]
        perm = [(ring[i], ring[(i + 1) % n]) for i in range(n)]
        plans.append((r * n * chunk, p, perm))

    def piece(plan, k):
        base, p, _ = plan
        return lax.dynamic_slice_in_dim(x, base + ((p - k) % n) * chunk, chunk, axis=1)

    accs = [piece(plan, 0) for plan in plans]
    for k in range(n - 1):
        accs = [lax.ppermute(acc, axis, plan[2]) + piece(plan, k + 1) for acc, plan in zip(accs, plans)]
    accs = [acc * scale for acc in accs]
    out = jnp.zeros_like(x)

    def put(out, block, plan, k):
        base, p, _ = plan
        return lax.dynamic_update_slice_in_dim(out, block, base + ((p + k) % n) * chunk, axis=1)

    for acc, plan in zip(accs, plans):
        out = put(out, acc, plan, 1)
    curs = accs
    for k in range(n - 1):
        curs = [lax.ppermute(cur, axis, plan[2]) for cur, plan in zip(curs, plans)]
        if k == n // 2:
            curs, hold = lax.optimization_barrier((curs, hold))
        for cur, plan in zip(curs, plans):
            out = put(out, cur, plan, -k)
    return out, hold


def shards(inputs, grad_out, weights):
    planes, ny, nz, fshare = grad_out.shape
    cin = weights.shape[3]
    voxels = planes * ny * nz
    scale = 1.0 / math.sqrt(voxels * lax.axis_size("space"))
    grad_rimmed = extended(grad_out, (("space", 0),), 1)
    grad_padded = jnp.pad(grad_rimmed, ((0, 0), (1, 1), (1, 1), (0, 0)))
    gathered = lax.all_gather(inputs, "filt", axis=3, tiled=True)
    width = gathered.shape[3]
    in_flat = gathered.reshape(voxels, width)
    rows_list = []
    for tap_a in range(3):
        for b in range(3):
            for c in range(3):
                moved = grad_padded[
                    2 - tap_a : 2 - tap_a + planes, 2 - b : 2 - b + ny, 2 - c : 2 - c + nz, :
                ].reshape(voxels, fshare)
                rows_list.append(
                    lax.dot_general(
                        in_flat,
                        moved,
                        (((0,), (0,)), ((), ())),
                        preferred_element_type=jnp.float32,
                    )
                )
    tap_sums = jnp.stack(rows_list)
    tap_sums, grad_padded, weights = lax.optimization_barrier((tap_sums, grad_padded, weights))
    data_term = jnp.zeros((voxels, cin), jnp.float32)
    for a in range(3):
        moved_list = []
        for data_b in range(3):
            for data_c in range(3):
                moved_list.append(
                    grad_padded[
                        2 - a : 2 - a + planes,
                        2 - data_b : 2 - data_b + ny,
                        2 - data_c : 2 - data_c + nz,
                        :,
                    ].reshape(voxels, fshare)
                )
        stacked = jnp.stack(moved_list, axis=1).reshape(voxels, 3, 3, fshare)
        data_term = data_term + lax.dot_general(
            stacked,
            weights[a],
            (((1, 2, 3), (0, 1, 3)), ((), ())),
            preferred_element_type=jnp.float32,
        )
    grad_inputs = lax.psum_scatter(
        data_term.reshape(planes, ny, nz, cin), "filt", scatter_dimension=3, tiled=True
    ).astype(jnp.bfloat16)
    summed, grad_inputs = ring_sum(tap_sums, "space", scale, grad_inputs)
    weight_grad = summed.reshape(3, 3, 3, width, fshare)
    return (grad_inputs, weight_grad)


def solution(mesh):
    placed = (
        P("space", None, None, "filt"),
        P("space", None, None, "filt"),
        P(None, None, None, None, "filt"),
    )
    return jax.shard_map(
        shards,
        mesh=mesh,
        in_specs=placed,
        out_specs=(P("space", None, None, "filt"), P(None, None, None, None, "filt")),
        check_vma=False,
    )
```

```python
import math

import jax
import jax.numpy as jnp
import numpy as np
from jax import lax
from jax.sharding import PartitionSpec as P


def extended(array, sides, width):
    for axis, dim in sides:
        size, length = (lax.axis_size(axis), array.shape[dim])
        up = [(i, (i + 1) % size) for i in range(size - 1)]
        down = [(j, i) for i, j in up]
        last = lax.slice_in_dim(array, length - width, length, axis=dim)
        first = lax.slice_in_dim(array, 0, width, axis=dim)
        before = lax.ppermute(last, axis, up)
        after = lax.ppermute(first, axis, down)
        array = jnp.concatenate([before, array, after], axis=dim)
    return array


def ring_order(n):
    if n % 2:
        return list(range(n))
    return list(range(0, n, 2)) + list(range(n - 1, 0, -2))


def ring_sum_dir(x, axis, order, base, chunk, scale, hold):
    n = len(order)
    pos_tab = np.zeros(n, np.int32)
    for i, s in enumerate(order):
        pos_tab[s] = i
    p = jnp.asarray(pos_tab)[lax.axis_index(axis)]
    perm = [(order[i], order[(i + 1) % n]) for i in range(n)]

    def piece(k):
        return lax.dynamic_slice_in_dim(x, base + ((p - k) % n) * chunk, chunk, axis=0)

    acc = piece(0)
    for k in range(n - 1):
        acc = lax.ppermute(acc, axis, perm) + piece(k + 1)
    acc = acc * scale
    out = jnp.zeros((n * chunk,) + x.shape[1:], x.dtype)
    out = lax.dynamic_update_slice_in_dim(out, acc, ((p + 1) % n) * chunk, axis=0)
    cur = acc
    for k in range(n - 1):
        cur = lax.ppermute(cur, axis, perm)
        if k == n // 2 and hold is not None:
            cur, hold = lax.optimization_barrier((cur, hold))
        out = lax.dynamic_update_slice_in_dim(out, cur, ((p - k) % n) * chunk, axis=0)
    return out, hold


def ring_sum(x, axis, scale, hold):
    n = lax.axis_size(axis)
    rows = x.shape[0]
    if n == 1 or rows % (16 * n):
        return lax.psum(x, axis) * scale, hold
    order = ring_order(n)
    chunk = rows // (2 * n)
    half = rows // 2
    first, hold = ring_sum_dir(x, axis, order, 0, chunk, scale, hold)
    second, _ = ring_sum_dir(x, axis, order[::-1], half, chunk, scale, None)
    return jnp.concatenate([first, second], axis=0), hold


def shards(inputs, grad_out, weights):
    planes, ny, nz, fshare = grad_out.shape
    cin = weights.shape[3]
    voxels = planes * ny * nz
    scale = 1.0 / math.sqrt(voxels * lax.axis_size("space"))
    grad_rimmed = extended(grad_out, (("space", 0),), 1)
    grad_padded = jnp.pad(grad_rimmed, ((0, 0), (1, 1), (1, 1), (0, 0)))
    gathered = lax.all_gather(inputs, "filt", axis=3, tiled=True)
    width = gathered.shape[3]
    data_term = jnp.zeros((voxels, cin), jnp.float32)
    for a in (1, 0, 2):
        moved_list = []
        for data_b in range(3):
            for data_c in range(3):
                moved_list.append(
                    grad_padded[
                        2 - a : 2 - a + planes,
                        2 - data_b : 2 - data_b + ny,
                        2 - data_c : 2 - data_c + nz,
                        :,
                    ].reshape(voxels, fshare)
                )
        stacked = jnp.stack(moved_list, axis=1).reshape(voxels, 3, 3, fshare)
        data_term = data_term + lax.dot_general(
            stacked,
            weights[a],
            (((1, 2, 3), (0, 1, 3)), ((), ())),
            preferred_element_type=jnp.float32,
        )
    data_term, gathered = lax.optimization_barrier((data_term, gathered))
    grad_inputs = lax.psum_scatter(
        data_term.reshape(planes, ny, nz, cin), "filt", scatter_dimension=3, tiled=True
    ).astype(jnp.bfloat16)
    in_flat = gathered.reshape(voxels, width)
    rows_list = []
    for tap_a in range(3):
        for b in range(3):
            for c in range(3):
                moved = grad_padded[
                    2 - tap_a : 2 - tap_a + planes, 2 - b : 2 - b + ny, 2 - c : 2 - c + nz, :
                ].reshape(voxels, fshare)
                rows_list.append(
                    lax.dot_general(
                        in_flat,
                        moved,
                        (((0,), (0,)), ((), ())),
                        preferred_element_type=jnp.float32,
                    )
                )
    tap_sums = jnp.stack(rows_list).reshape(27 * width, fshare)
    summed, grad_inputs = ring_sum(tap_sums, "space", scale, grad_inputs)
    weight_grad = summed.reshape(3, 3, 3, width, fshare)
    return (grad_inputs, weight_grad)


def solution(mesh):
    placed = (
        P("space", None, None, "filt"),
        P("space", None, None, "filt"),
        P(None, None, None, None, "filt"),
    )
    return jax.shard_map(
        shards,
        mesh=mesh,
        in_specs=placed,
        out_specs=(P("space", None, None, "filt"), P(None, None, None, None, "filt")),
        check_vma=False,
    )
```

```python
import math

import jax
import jax.numpy as jnp
import numpy as np
from jax import lax
from jax.experimental import pallas as pl
from jax.experimental.pallas import tpu as pltpu
from jax.sharding import PartitionSpec as P


def extended(array, sides, width):
    for axis, dim in sides:
        size, length = (lax.axis_size(axis), array.shape[dim])
        up = [(i, (i + 1) % size) for i in range(size - 1)]
        down = [(j, i) for i, j in up]
        last = lax.slice_in_dim(array, length - width, length, axis=dim)
        first = lax.slice_in_dim(array, 0, width, axis=dim)
        before = lax.ppermute(last, axis, up)
        after = lax.ppermute(first, axis, down)
        array = jnp.concatenate([before, array, after], axis=dim)
    return array


def wgrad_kernel(int_ref, g0_ref, g1_ref, g2_ref, out_ref):
    a = pl.program_id(0)
    b = pl.program_id(1)
    planes = g0_ref.shape[0] - 2
    ny = g0_ref.shape[1] - 2
    for c, g_ref in enumerate((g0_ref, g1_ref, g2_ref)):
        win = g_ref[pl.ds(2 - a, planes), pl.ds(2 - b, ny), :, :]
        moved = win.reshape(-1, win.shape[-1])
        out_ref[c] = jnp.dot(int_ref[...], moved, preferred_element_type=jnp.float32)

def weight_taps(in_t, grad_padded):
    planes2, ny2, nz2, fshare = grad_padded.shape
    nz = nz2 - 2
    width, voxels = in_t.shape
    shifted = [grad_padded[:, :, 2 - c : 2 - c + nz, :] for c in range(3)]
    full = lambda shape: pl.BlockSpec(shape, lambda a, b: (0,) * len(shape))
    return pl.pallas_call(
        wgrad_kernel,
        grid=(3, 3),
        in_specs=[full(in_t.shape)] + [full(s.shape) for s in shifted],
        out_specs=pl.BlockSpec((3, width, fshare), lambda a, b: (a * 3 + b, 0, 0)),
        out_shape=jax.ShapeDtypeStruct((27, width, fshare), jnp.float32),
        compiler_params=pltpu.CompilerParams(vmem_limit_bytes=48 * 1024 * 1024),
        cost_estimate=pl.CostEstimate(flops=2 * 27 * width * voxels * fshare, transcendentals=0,
                                      bytes_accessed=in_t.size * 2 + 3 * shifted[0].size * 2 + 27 * width * fshare * 4),
    )(in_t, *shifted)

def ring_order(n):
    if n % 2:
        return list(range(n))
    return list(range(0, n, 2)) + list(range(n - 1, 0, -2))


def ring_sum_dir(x, axis, order, base, chunk, scale, hold):
    n = len(order)
    pos_tab = np.zeros(n, np.int32)
    for i, s in enumerate(order):
        pos_tab[s] = i
    p = jnp.asarray(pos_tab)[lax.axis_index(axis)]
    perm = [(order[i], order[(i + 1) % n]) for i in range(n)]

    def piece(k):
        start = base + ((p - k) % n) * chunk
        return lax.dynamic_slice_in_dim(x, start, chunk, axis=1)

    acc = piece(0)
    for k in range(n - 1):
        acc = lax.ppermute(acc, axis, perm) + piece(k + 1)
    acc = acc * scale
    out = jnp.zeros(x.shape[:1] + (n * chunk,) + x.shape[2:], x.dtype)
    out = lax.dynamic_update_slice_in_dim(out, acc, ((p + 1) % n) * chunk, axis=1)
    cur = acc
    for k in range(n - 1):
        cur = lax.ppermute(cur, axis, perm)
        if k == n // 2 and hold is not None:
            cur, hold = lax.optimization_barrier((cur, hold))
        out = lax.dynamic_update_slice_in_dim(out, cur, ((p - k) % n) * chunk, axis=1)
    return out, hold


def ring_sum(x, axis, scale, hold):
    n = lax.axis_size(axis)
    rows = x.shape[1]
    if n == 1 or rows % (16 * n):
        return lax.psum(x, axis) * scale, hold
    order = ring_order(n)
    chunk = rows // (2 * n)
    half = rows // 2
    first, hold = ring_sum_dir(x, axis, order, 0, chunk, scale, hold)
    second, _ = ring_sum_dir(x, axis, order[::-1], half, chunk, scale, None)
    return jnp.concatenate([first, second], axis=1), hold


def shards(inputs, grad_out, weights):
    planes, ny, nz, fshare = grad_out.shape
    cin = weights.shape[3]
    voxels = planes * ny * nz
    scale = 1.0 / math.sqrt(voxels * lax.axis_size("space"))
    grad_rimmed = extended(grad_out, (("space", 0),), 1)
    grad_padded = jnp.pad(grad_rimmed, ((0, 0), (1, 1), (1, 1), (0, 0)))
    gathered = lax.all_gather(inputs, "filt", axis=3, tiled=True)
    width = gathered.shape[3]
    data_term = jnp.zeros((voxels, cin), jnp.float32)
    for a in (1, 0, 2):
        moved_list = []
        for data_b in range(3):
            for data_c in range(3):
                moved_list.append(
                    grad_padded[
                        2 - a : 2 - a + planes,
                        2 - data_b : 2 - data_b + ny,
                        2 - data_c : 2 - data_c + nz,
                        :,
                    ].reshape(voxels, fshare)
                )
        stacked = jnp.stack(moved_list, axis=1).reshape(voxels, 3, 3, fshare)
        data_term = data_term + lax.dot_general(
            stacked,
            weights[a],
            (((1, 2, 3), (0, 1, 3)), ((), ())),
            preferred_element_type=jnp.float32,
        )
    data_term, gathered = lax.optimization_barrier((data_term, gathered))
    grad_inputs = lax.psum_scatter(
        data_term.reshape(planes, ny, nz, cin), "filt", scatter_dimension=3, tiled=True
    ).astype(jnp.bfloat16)
    in_t = gathered.reshape(voxels, width).T
    tap_sums = weight_taps(in_t, grad_padded)
    summed, grad_inputs = ring_sum(tap_sums, "space", scale, grad_inputs)
    weight_grad = summed.reshape(3, 3, 3, width, fshare)
    return (grad_inputs, weight_grad)


def solution(mesh):
    placed = (
        P("space", None, None, "filt"),
        P("space", None, None, "filt"),
        P(None, None, None, None, "filt"),
    )
    return jax.shard_map(
        shards,
        mesh=mesh,
        in_specs=placed,
        out_specs=(P("space", None, None, "filt"), P(None, None, None, None, "filt")),
        check_vma=False,
    )
```

```python
import math

import jax
import jax.numpy as jnp
import numpy as np
from jax import lax
from jax.experimental import pallas as pl
from jax.experimental.pallas import tpu as pltpu
from jax.sharding import PartitionSpec as P


def extended(array, sides, width):
    for axis, dim in sides:
        size, length = (lax.axis_size(axis), array.shape[dim])
        up = [(i, (i + 1) % size) for i in range(size - 1)]
        down = [(j, i) for i, j in up]
        last = lax.slice_in_dim(array, length - width, length, axis=dim)
        first = lax.slice_in_dim(array, 0, width, axis=dim)
        before = lax.ppermute(last, axis, up)
        after = lax.ppermute(first, axis, down)
        array = jnp.concatenate([before, array, after], axis=dim)
    return array


def wgrad_kernel(int_ref, g0_ref, g1_ref, g2_ref, out_ref):
    a = pl.program_id(0)
    b = pl.program_id(1)
    planes = g0_ref.shape[0] - 2
    ny = g0_ref.shape[1] - 2
    for c, g_ref in enumerate((g0_ref, g1_ref, g2_ref)):
        win = g_ref[pl.ds(2 - a, planes), pl.ds(2 - b, ny), :, :]
        moved = win.reshape(-1, win.shape[-1])
        out_ref[c] = jnp.dot(int_ref[...], moved, preferred_element_type=jnp.float32)

def weight_taps(in_t, grad_padded):
    planes2, ny2, nz2, fshare = grad_padded.shape
    nz = nz2 - 2
    width, voxels = in_t.shape
    shifted = [grad_padded[:, :, 2 - c : 2 - c + nz, :] for c in range(3)]
    full = lambda shape: pl.BlockSpec(shape, lambda a, b: (0,) * len(shape))
    return pl.pallas_call(
        wgrad_kernel,
        grid=(3, 3),
        in_specs=[full(in_t.shape)] + [full(s.shape) for s in shifted],
        out_specs=pl.BlockSpec((3, width, fshare), lambda a, b: (a * 3 + b, 0, 0)),
        out_shape=jax.ShapeDtypeStruct((27, width, fshare), jnp.float32),
        compiler_params=pltpu.CompilerParams(vmem_limit_bytes=48 * 1024 * 1024),
        cost_estimate=pl.CostEstimate(flops=2 * 27 * width * voxels * fshare, transcendentals=0,
                                      bytes_accessed=in_t.size * 2 + 3 * shifted[0].size * 2 + 27 * width * fshare * 4),
    )(in_t, *shifted)

def ring_order(n):
    if n % 2:
        return list(range(n))
    return list(range(0, n, 2)) + list(range(n - 1, 0, -2))


def ring_sum_dir(x, axis, order, base, chunk, scale, hold):
    n = len(order)
    pos_tab = np.zeros(n, np.int32)
    for i, s in enumerate(order):
        pos_tab[s] = i
    p = jnp.asarray(pos_tab)[lax.axis_index(axis)]
    perm = [(order[i], order[(i + 1) % n]) for i in range(n)]

    def piece(k):
        start = base + ((p - k) % n) * chunk
        return lax.dynamic_slice_in_dim(x, start, chunk, axis=1)

    acc = piece(0)
    for k in range(n - 1):
        acc = lax.ppermute(acc, axis, perm) + piece(k + 1)
    acc = acc * scale
    got = [acc]
    cur = acc
    for k in range(n - 1):
        cur = lax.ppermute(cur, axis, perm)
        if k == n // 2 and hold is not None:
            cur, hold = lax.optimization_barrier((cur, hold))
        got.append(cur)
    rev = jnp.stack(got[::-1])
    double = jnp.concatenate([rev, rev], axis=0)
    placed = lax.dynamic_slice_in_dim(double, (-p - 2) % n, n, axis=0)
    return jnp.moveaxis(placed, 0, 1).reshape(x.shape[0], n * chunk, *x.shape[2:]), hold


def ring_sum(x, axis, scale, hold):
    n = lax.axis_size(axis)
    rows = x.shape[1]
    if n == 1 or rows % (16 * n):
        return lax.psum(x, axis) * scale, hold
    order = ring_order(n)
    chunk = rows // (2 * n)
    half = rows // 2
    first, hold = ring_sum_dir(x, axis, order, 0, chunk, scale, hold)
    second, _ = ring_sum_dir(x, axis, order[::-1], half, chunk, scale, None)
    return jnp.concatenate([first, second], axis=1), hold


def shards(inputs, grad_out, weights):
    planes, ny, nz, fshare = grad_out.shape
    cin = weights.shape[3]
    voxels = planes * ny * nz
    scale = 1.0 / math.sqrt(voxels * lax.axis_size("space"))
    grad_rimmed = extended(grad_out, (("space", 0),), 1)
    grad_padded = jnp.pad(grad_rimmed, ((0, 0), (1, 1), (1, 1), (0, 0)))
    gathered = lax.all_gather(inputs, "filt", axis=3, tiled=True)
    width = gathered.shape[3]
    data_term = jnp.zeros((voxels, cin), jnp.float32)
    for a in (1, 0, 2):
        moved_list = []
        for data_b in range(3):
            for data_c in range(3):
                moved_list.append(
                    grad_padded[
                        2 - a : 2 - a + planes,
                        2 - data_b : 2 - data_b + ny,
                        2 - data_c : 2 - data_c + nz,
                        :,
                    ].reshape(voxels, fshare)
                )
        stacked = jnp.stack(moved_list, axis=1).reshape(voxels, 3, 3, fshare)
        data_term = data_term + lax.dot_general(
            stacked,
            weights[a],
            (((1, 2, 3), (0, 1, 3)), ((), ())),
            preferred_element_type=jnp.float32,
        )
    data_term, gathered = lax.optimization_barrier((data_term, gathered))
    grad_inputs = lax.psum_scatter(
        data_term.reshape(planes, ny, nz, cin), "filt", scatter_dimension=3, tiled=True
    ).astype(jnp.bfloat16)
    in_t = gathered.reshape(voxels, width).T
    tap_sums = weight_taps(in_t, grad_padded)
    summed, grad_inputs = ring_sum(tap_sums, "space", scale, grad_inputs)
    weight_grad = summed.reshape(3, 3, 3, width, fshare)
    return (grad_inputs, weight_grad)


def solution(mesh):
    placed = (
        P("space", None, None, "filt"),
        P("space", None, None, "filt"),
        P(None, None, None, None, "filt"),
    )
    return jax.shard_map(
        shards,
        mesh=mesh,
        in_specs=placed,
        out_specs=(P("space", None, None, "filt"), P(None, None, None, None, "filt")),
        check_vma=False,
    )
```

```python
import math

import jax
import jax.numpy as jnp
import numpy as np
from jax import lax
from jax.experimental import pallas as pl
from jax.experimental.pallas import tpu as pltpu
from jax.sharding import PartitionSpec as P


def extended(array, sides, width):
    for axis, dim in sides:
        size, length = (lax.axis_size(axis), array.shape[dim])
        up = [(i, (i + 1) % size) for i in range(size - 1)]
        down = [(j, i) for i, j in up]
        last = lax.slice_in_dim(array, length - width, length, axis=dim)
        first = lax.slice_in_dim(array, 0, width, axis=dim)
        before = lax.ppermute(last, axis, up)
        after = lax.ppermute(first, axis, down)
        array = jnp.concatenate([before, array, after], axis=dim)
    return array


def wgrad_kernel(int_ref, g0_ref, g1_ref, g2_ref, out_ref):
    a = pl.program_id(0)
    b = pl.program_id(1)
    planes = g0_ref.shape[0] - 2
    ny = g0_ref.shape[1] - 2
    for c, g_ref in enumerate((g0_ref, g1_ref, g2_ref)):
        win = g_ref[pl.ds(2 - a, planes), pl.ds(2 - b, ny), :, :]
        moved = win.reshape(-1, win.shape[-1])
        out_ref[c] = jnp.dot(int_ref[...], moved, preferred_element_type=jnp.float32)

def weight_taps(in_t, grad_padded):
    planes2, ny2, nz2, fshare = grad_padded.shape
    nz = nz2 - 2
    width, voxels = in_t.shape
    shifted = [grad_padded[:, :, 2 - c : 2 - c + nz, :] for c in range(3)]
    full = lambda shape: pl.BlockSpec(shape, lambda a, b: (0,) * len(shape))
    return pl.pallas_call(
        wgrad_kernel,
        grid=(3, 3),
        in_specs=[full(in_t.shape)] + [full(s.shape) for s in shifted],
        out_specs=pl.BlockSpec((3, width, fshare), lambda a, b: (a * 3 + b, 0, 0)),
        out_shape=jax.ShapeDtypeStruct((27, width, fshare), jnp.float32),
        compiler_params=pltpu.CompilerParams(vmem_limit_bytes=48 * 1024 * 1024),
        cost_estimate=pl.CostEstimate(flops=2 * 27 * width * voxels * fshare, transcendentals=0,
                                      bytes_accessed=in_t.size * 2 + 3 * shifted[0].size * 2 + 27 * width * fshare * 4),
    )(in_t, *shifted)

def ring_order(n):
    if n % 2:
        return list(range(n))
    return list(range(0, n, 2)) + list(range(n - 1, 0, -2))


def ring_sum_dir(x, axis, order, base, chunk, scale, hold):
    n = len(order)
    pos_tab = np.zeros(n, np.int32)
    for i, s in enumerate(order):
        pos_tab[s] = i
    p = jnp.asarray(pos_tab)[lax.axis_index(axis)]
    perm = [(order[i], order[(i + 1) % n]) for i in range(n)]

    def piece(k):
        start = base + ((p - k) % n) * chunk
        return lax.dynamic_slice_in_dim(x, start, chunk, axis=1)

    acc = piece(0)
    for k in range(n - 1):
        acc = lax.ppermute(acc, axis, perm) + piece(k + 1)
    acc = acc * scale
    out = jnp.zeros(x.shape[:1] + (n * chunk,) + x.shape[2:], x.dtype)
    out = lax.dynamic_update_slice_in_dim(out, acc, ((p + 1) % n) * chunk, axis=1)
    cur = acc
    for k in range(n - 1):
        cur = lax.ppermute(cur, axis, perm)
        if k == n // 2 and hold is not None:
            cur, hold = lax.optimization_barrier((cur, hold))
        out = lax.dynamic_update_slice_in_dim(out, cur, ((p - k) % n) * chunk, axis=1)
    return out, hold


def ring_sum(halves, axis, scale, hold):
    n = lax.axis_size(axis)
    rows = halves[0].shape[1]
    if n == 1 or rows % (8 * n):
        return lax.psum(jnp.concatenate(halves, axis=1), axis) * scale, hold
    order = ring_order(n)
    chunk = rows // n
    first, hold = ring_sum_dir(halves[0], axis, order, 0, chunk, scale, hold)
    second, _ = ring_sum_dir(halves[1], axis, order[::-1], 0, chunk, scale, None)
    return jnp.concatenate([first, second], axis=1), hold


def shards(inputs, grad_out, weights):
    planes, ny, nz, fshare = grad_out.shape
    cin = weights.shape[3]
    voxels = planes * ny * nz
    scale = 1.0 / math.sqrt(voxels * lax.axis_size("space"))
    grad_rimmed = extended(grad_out, (("space", 0),), 1)
    grad_padded = jnp.pad(grad_rimmed, ((0, 0), (1, 1), (1, 1), (0, 0)))
    gathered = lax.all_gather(inputs, "filt", axis=3, tiled=True)
    width = gathered.shape[3]
    data_term = jnp.zeros((voxels, cin), jnp.float32)
    for a in (1, 0, 2):
        moved_list = []
        for data_b in range(3):
            for data_c in range(3):
                moved_list.append(
                    grad_padded[
                        2 - a : 2 - a + planes,
                        2 - data_b : 2 - data_b + ny,
                        2 - data_c : 2 - data_c + nz,
                        :,
                    ].reshape(voxels, fshare)
                )
        stacked = jnp.stack(moved_list, axis=1).reshape(voxels, 3, 3, fshare)
        data_term = data_term + lax.dot_general(
            stacked,
            weights[a],
            (((1, 2, 3), (0, 1, 3)), ((), ())),
            preferred_element_type=jnp.float32,
        )
    data_term, gathered = lax.optimization_barrier((data_term, gathered))
    grad_inputs = lax.psum_scatter(
        data_term.reshape(planes, ny, nz, cin), "filt", scatter_dimension=3, tiled=True
    ).astype(jnp.bfloat16)
    in_t = gathered.reshape(voxels, width).T
    half = width // 2
    halves = [weight_taps(in_t[:half], grad_padded), weight_taps(in_t[half:], grad_padded)]
    summed, grad_inputs = ring_sum(halves, "space", scale, grad_inputs)
    weight_grad = summed.reshape(3, 3, 3, width, fshare)
    return (grad_inputs, weight_grad)


def solution(mesh):
    placed = (
        P("space", None, None, "filt"),
        P("space", None, None, "filt"),
        P(None, None, None, None, "filt"),
    )
    return jax.shard_map(
        shards,
        mesh=mesh,
        in_specs=placed,
        out_specs=(P("space", None, None, "filt"), P(None, None, None, None, "filt")),
        check_vma=False,
    )
```

```python
import math

import jax
import jax.numpy as jnp
import numpy as np
from jax import lax
from jax.experimental import pallas as pl
from jax.experimental.pallas import tpu as pltpu
from jax.sharding import PartitionSpec as P


def extended(array, sides, width):
    for axis, dim in sides:
        size, length = (lax.axis_size(axis), array.shape[dim])
        up = [(i, (i + 1) % size) for i in range(size - 1)]
        down = [(j, i) for i, j in up]
        last = lax.slice_in_dim(array, length - width, length, axis=dim)
        first = lax.slice_in_dim(array, 0, width, axis=dim)
        before = lax.ppermute(last, axis, up)
        after = lax.ppermute(first, axis, down)
        array = jnp.concatenate([before, array, after], axis=dim)
    return array


def wgrad_kernel(int_ref, g0_ref, g1_ref, g2_ref, out_ref):
    a = pl.program_id(0)
    b = pl.program_id(1)
    planes = g0_ref.shape[0] - 2
    ny = g0_ref.shape[1] - 2
    for c, g_ref in enumerate((g0_ref, g1_ref, g2_ref)):
        win = g_ref[pl.ds(2 - a, planes), pl.ds(2 - b, ny), :, :]
        moved = win.reshape(-1, win.shape[-1])
        out_ref[c] = lax.dot_general(
            int_ref[...], moved, (((0,), (0,)), ((), ())), preferred_element_type=jnp.float32
        )

def weight_taps(in_t, grad_padded, part, parts):
    planes2, ny2, nz2, fshare = grad_padded.shape
    nz = nz2 - 2
    voxels, width = in_t.shape
    width //= parts
    shifted = [grad_padded[:, :, 2 - c : 2 - c + nz, :] for c in range(3)]
    full = lambda shape: pl.BlockSpec(shape, lambda a, b: (0,) * len(shape))
    return pl.pallas_call(
        wgrad_kernel,
        grid=(3, 3),
        in_specs=[pl.BlockSpec((voxels, width), lambda a, b: (0, part))]
        + [full(s.shape) for s in shifted],
        out_specs=pl.BlockSpec((3, width, fshare), lambda a, b: (a * 3 + b, 0, 0)),
        out_shape=jax.ShapeDtypeStruct((27, width, fshare), jnp.float32),
        compiler_params=pltpu.CompilerParams(vmem_limit_bytes=48 * 1024 * 1024),
        cost_estimate=pl.CostEstimate(flops=2 * 27 * width * voxels * fshare, transcendentals=0,
                                      bytes_accessed=voxels * width * 2 + 3 * shifted[0].size * 2 + 27 * width * fshare * 4),
    )(in_t, *shifted)

def ring_order(n):
    if n % 2:
        return list(range(n))
    return list(range(0, n, 2)) + list(range(n - 1, 0, -2))


def ring_sum(halves, axis, scale, hold):
    n = lax.axis_size(axis)
    rows = halves[0].shape[1]
    if n == 1 or rows % (8 * n):
        return lax.psum(jnp.concatenate(halves, axis=1), axis) * scale, hold
    order = ring_order(n)
    chunk = rows // n
    plans = []
    for r, ring in enumerate((order, order[::-1])):
        pos_tab = np.zeros(n, np.int32)
        for i, dev in enumerate(ring):
            pos_tab[dev] = i
        p = jnp.asarray(pos_tab)[lax.axis_index(axis)]
        perm = [(ring[i], ring[(i + 1) % n]) for i in range(n)]
        plans.append((r * rows, p, perm))

    def piece(x, p, k):
        return lax.dynamic_slice_in_dim(x, ((p - k) % n) * chunk, chunk, axis=1)

    accs = []
    for x, (_, p, perm) in zip(halves, plans):
        acc = piece(x, p, 0)
        for k in range(n - 1):
            acc = lax.ppermute(acc, axis, perm) + piece(x, p, k + 1)
        accs.append(acc * scale)
    x = halves[0]
    out = jnp.zeros((x.shape[0], 2 * rows, x.shape[2]), x.dtype)
    for acc, (base, p, _) in zip(accs, plans):
        out = lax.dynamic_update_slice_in_dim(out, acc, base + ((p + 1) % n) * chunk, axis=1)
    curs = accs
    for k in range(n - 1):
        curs = [lax.ppermute(cur, axis, plan[2]) for cur, plan in zip(curs, plans)]
        if k == n // 2:
            curs, hold = lax.optimization_barrier((curs, hold))
        for cur, (base, p, _) in zip(curs, plans):
            out = lax.dynamic_update_slice_in_dim(out, cur, base + ((p - k) % n) * chunk, axis=1)
    return out, hold


def shards(inputs, grad_out, weights):
    planes, ny, nz, fshare = grad_out.shape
    cin = weights.shape[3]
    voxels = planes * ny * nz
    scale = 1.0 / math.sqrt(voxels * lax.axis_size("space"))
    grad_rimmed = extended(grad_out, (("space", 0),), 1)
    grad_padded = jnp.pad(grad_rimmed, ((0, 0), (1, 1), (1, 1), (0, 0)))
    gathered = lax.all_gather(inputs, "filt", axis=3, tiled=True)
    width = gathered.shape[3]
    data_term = jnp.zeros((voxels, cin), jnp.float32)
    for a in (1, 0, 2):
        moved_list = []
        for data_b in range(3):
            for data_c in range(3):
                moved_list.append(
                    grad_padded[
                        2 - a : 2 - a + planes,
                        2 - data_b : 2 - data_b + ny,
                        2 - data_c : 2 - data_c + nz,
                        :,
                    ].reshape(voxels, fshare)
                )
        stacked = jnp.stack(moved_list, axis=1).reshape(voxels, 3, 3, fshare)
        data_term = data_term + lax.dot_general(
            stacked,
            weights[a],
            (((1, 2, 3), (0, 1, 3)), ((), ())),
            preferred_element_type=jnp.float32,
        )
    data_term, gathered = lax.optimization_barrier((data_term, gathered))
    grad_inputs = lax.psum_scatter(
        data_term.reshape(planes, ny, nz, cin), "filt", scatter_dimension=3, tiled=True
    ).astype(jnp.bfloat16)
    in_t = gathered.reshape(voxels, width)
    halves = [weight_taps(in_t, grad_padded, 0, 2), weight_taps(in_t, grad_padded, 1, 2)]
    summed, grad_inputs = ring_sum(halves, "space", scale, grad_inputs)
    weight_grad = summed.reshape(3, 3, 3, width, fshare)
    return (grad_inputs, weight_grad)


def solution(mesh):
    placed = (
        P("space", None, None, "filt"),
        P("space", None, None, "filt"),
        P(None, None, None, None, "filt"),
    )
    return jax.shard_map(
        shards,
        mesh=mesh,
        in_specs=placed,
        out_specs=(P("space", None, None, "filt"), P(None, None, None, None, "filt")),
        check_vma=False,
    )
```

```python
import math

import jax
import jax.numpy as jnp
import numpy as np
from jax import lax
from jax.experimental import pallas as pl
from jax.experimental.pallas import tpu as pltpu
from jax.sharding import PartitionSpec as P


def extended(array, sides, width):
    for axis, dim in sides:
        size, length = (lax.axis_size(axis), array.shape[dim])
        up = [(i, (i + 1) % size) for i in range(size - 1)]
        down = [(j, i) for i, j in up]
        last = lax.slice_in_dim(array, length - width, length, axis=dim)
        first = lax.slice_in_dim(array, 0, width, axis=dim)
        before = lax.ppermute(last, axis, up)
        after = lax.ppermute(first, axis, down)
        array = jnp.concatenate([before, array, after], axis=dim)
    return array


def wgrad_kernel(int_ref, g0_ref, g1_ref, g2_ref, out_ref):
    a = pl.program_id(0)
    b = pl.program_id(1)
    planes = g0_ref.shape[0] - 2
    ny = g0_ref.shape[1] - 2
    for c, g_ref in enumerate((g0_ref, g1_ref, g2_ref)):
        win = g_ref[pl.ds(2 - a, planes), pl.ds(2 - b, ny), :, :]
        moved = win.reshape(-1, win.shape[-1])
        out_ref[c] = lax.dot_general(
            int_ref[...], moved, (((0,), (0,)), ((), ())), preferred_element_type=jnp.float32
        )

def weight_taps(in_t, grad_padded, part, parts):
    planes2, ny2, nz2, fshare = grad_padded.shape
    nz = nz2 - 2
    voxels, width = in_t.shape
    width //= parts
    shifted = [grad_padded[:, :, 2 - c : 2 - c + nz, :] for c in range(3)]
    full = lambda shape: pl.BlockSpec(shape, lambda a, b: (0,) * len(shape))
    return pl.pallas_call(
        wgrad_kernel,
        grid=(3, 3),
        in_specs=[pl.BlockSpec((voxels, width), lambda a, b: (0, part))]
        + [full(s.shape) for s in shifted],
        out_specs=pl.BlockSpec((3, width, fshare), lambda a, b: (a * 3 + b, 0, 0)),
        out_shape=jax.ShapeDtypeStruct((27, width, fshare), jnp.float32),
        compiler_params=pltpu.CompilerParams(vmem_limit_bytes=48 * 1024 * 1024),
        cost_estimate=pl.CostEstimate(flops=2 * 27 * width * voxels * fshare, transcendentals=0,
                                      bytes_accessed=voxels * width * 2 + 3 * shifted[0].size * 2 + 27 * width * fshare * 4),
    )(in_t, *shifted)

def ring_order(n):
    if n % 2:
        return list(range(n))
    return list(range(0, n, 2)) + list(range(n - 1, 0, -2))


def ring_sum(halves, bases, axis, scale, hold):
    n = lax.axis_size(axis)
    rows = halves[0].shape[1]
    if n == 1 or rows % (8 * n):
        x = halves[0]
        out = jnp.zeros((x.shape[0], 2 * rows, x.shape[2]), x.dtype)
        for half, base in zip(halves, bases):
            out = lax.dynamic_update_slice_in_dim(out, half, base, axis=1)
        return lax.psum(out, axis) * scale, hold
    order = ring_order(n)
    chunk = rows // n
    plans = []
    for r, ring in enumerate((order, order[::-1])):
        pos_tab = np.zeros(n, np.int32)
        for i, dev in enumerate(ring):
            pos_tab[dev] = i
        p = jnp.asarray(pos_tab)[lax.axis_index(axis)]
        perm = [(ring[i], ring[(i + 1) % n]) for i in range(n)]
        plans.append((bases[r], p, perm))

    def piece(x, p, k):
        return lax.dynamic_slice_in_dim(x, ((p - k) % n) * chunk, chunk, axis=1)

    accs = []
    for x, (_, p, perm) in zip(halves, plans):
        acc = piece(x, p, 0)
        for k in range(n - 1):
            acc = lax.ppermute(acc, axis, perm) + piece(x, p, k + 1)
        accs.append(acc * scale)
    x = halves[0]
    out = jnp.zeros((x.shape[0], 2 * rows, x.shape[2]), x.dtype)
    for acc, (base, p, _) in zip(accs, plans):
        out = lax.dynamic_update_slice_in_dim(out, acc, base + ((p + 1) % n) * chunk, axis=1)
    curs = accs
    for k in range(n - 1):
        curs = [lax.ppermute(cur, axis, plan[2]) for cur, plan in zip(curs, plans)]
        if k == n // 2:
            curs, hold = lax.optimization_barrier((curs, hold))
        for cur, (base, p, _) in zip(curs, plans):
            out = lax.dynamic_update_slice_in_dim(out, cur, base + ((p - k) % n) * chunk, axis=1)
    return out, hold


def shards(inputs, grad_out, weights):
    planes, ny, nz, fshare = grad_out.shape
    cin = weights.shape[3]
    voxels = planes * ny * nz
    scale = 1.0 / math.sqrt(voxels * lax.axis_size("space"))
    grad_rimmed = extended(grad_out, (("space", 0),), 1)
    grad_padded = jnp.pad(grad_rimmed, ((0, 0), (1, 1), (1, 1), (0, 0)))
    gathered = lax.all_gather(inputs, "filt", axis=3, tiled=True)
    width = gathered.shape[3]
    fsize = lax.axis_size("filt")
    f = lax.axis_index("filt")
    if fsize == 4:
        partner = lax.ppermute(inputs, "filt", [(i, i ^ 1) for i in range(fsize)])
        core, chip = f % 2, f // 2
        own_half = jnp.where(
            core == 0,
            jnp.concatenate([inputs, partner], axis=3),
            jnp.concatenate([partner, inputs], axis=3),
        )
        other_half = lax.dynamic_slice_in_dim(gathered, (1 - chip) * 2 * fshare, 2 * fshare, axis=3)
        bases = [chip * 2 * fshare, (1 - chip) * 2 * fshare]
    else:
        own_half = gathered[..., : width // 2]
        other_half = gathered[..., width // 2 :]
        bases = [0, width // 2]
    first = weight_taps(own_half.reshape(voxels, -1), grad_padded, 0, 1)
    second = weight_taps(other_half.reshape(voxels, -1), grad_padded, 0, 1)
    second, grad_padded, weights = lax.optimization_barrier((second, grad_padded, weights))
    data_term = jnp.zeros((voxels, cin), jnp.float32)
    for a in (1, 0, 2):
        moved_list = []
        for data_b in range(3):
            for data_c in range(3):
                moved_list.append(
                    grad_padded[
                        2 - a : 2 - a + planes,
                        2 - data_b : 2 - data_b + ny,
                        2 - data_c : 2 - data_c + nz,
                        :,
                    ].reshape(voxels, fshare)
                )
        stacked = jnp.stack(moved_list, axis=1).reshape(voxels, 3, 3, fshare)
        data_term = data_term + lax.dot_general(
            stacked,
            weights[a],
            (((1, 2, 3), (0, 1, 3)), ((), ())),
            preferred_element_type=jnp.float32,
        )
    grad_inputs = lax.psum_scatter(
        data_term.reshape(planes, ny, nz, cin), "filt", scatter_dimension=3, tiled=True
    ).astype(jnp.bfloat16)
    summed, grad_inputs = ring_sum([first, second], bases, "space", scale, grad_inputs)
    weight_grad = summed.reshape(3, 3, 3, width, fshare)
    return (grad_inputs, weight_grad)


def solution(mesh):
    placed = (
        P("space", None, None, "filt"),
        P("space", None, None, "filt"),
        P(None, None, None, None, "filt"),
    )
    return jax.shard_map(
        shards,
        mesh=mesh,
        in_specs=placed,
        out_specs=(P("space", None, None, "filt"), P(None, None, None, None, "filt")),
        check_vma=False,
    )
```

```python
import math

import jax
import jax.numpy as jnp
import numpy as np
from jax import lax
from jax.experimental import pallas as pl
from jax.experimental.pallas import tpu as pltpu
from jax.sharding import PartitionSpec as P


def extended(array, sides, width):
    for axis, dim in sides:
        size, length = (lax.axis_size(axis), array.shape[dim])
        up = [(i, (i + 1) % size) for i in range(size - 1)]
        down = [(j, i) for i, j in up]
        last = lax.slice_in_dim(array, length - width, length, axis=dim)
        first = lax.slice_in_dim(array, 0, width, axis=dim)
        before = lax.ppermute(last, axis, up)
        after = lax.ppermute(first, axis, down)
        array = jnp.concatenate([before, array, after], axis=dim)
    return array


def wgrad_kernel(int_ref, g0_ref, g1_ref, g2_ref, out_ref):
    a = pl.program_id(0)
    b = pl.program_id(1)
    planes = g0_ref.shape[0] - 2
    ny = g0_ref.shape[1] - 2
    for c, g_ref in enumerate((g0_ref, g1_ref, g2_ref)):
        win = g_ref[pl.ds(2 - a, planes), pl.ds(2 - b, ny), :, :]
        moved = win.reshape(-1, win.shape[-1])
        out_ref[c] = lax.dot_general(
            int_ref[...], moved, (((0,), (0,)), ((), ())), preferred_element_type=jnp.float32
        )

def weight_taps(in_t, grad_padded, part, parts):
    planes2, ny2, nz2, fshare = grad_padded.shape
    nz = nz2 - 2
    voxels, width = in_t.shape
    width //= parts
    shifted = [grad_padded[:, :, 2 - c : 2 - c + nz, :] for c in range(3)]
    full = lambda shape: pl.BlockSpec(shape, lambda a, b: (0,) * len(shape))
    return pl.pallas_call(
        wgrad_kernel,
        grid=(3, 3),
        in_specs=[pl.BlockSpec((voxels, width), lambda a, b: (0, part))]
        + [full(s.shape) for s in shifted],
        out_specs=pl.BlockSpec((3, width, fshare), lambda a, b: (a * 3 + b, 0, 0)),
        out_shape=jax.ShapeDtypeStruct((27, width, fshare), jnp.float32),
        compiler_params=pltpu.CompilerParams(vmem_limit_bytes=48 * 1024 * 1024),
        cost_estimate=pl.CostEstimate(flops=2 * 27 * width * voxels * fshare, transcendentals=0,
                                      bytes_accessed=voxels * width * 2 + 3 * shifted[0].size * 2 + 27 * width * fshare * 4),
    )(in_t, *shifted)

def ring_order(n):
    if n % 2:
        return list(range(n))
    return list(range(0, n, 2)) + list(range(n - 1, 0, -2))


def ring_sum(halves, bases, axis, scale, early, late_fn):
    n = lax.axis_size(axis)
    rows = halves[0].shape[1]
    if n == 1 or rows % (8 * n):
        x = halves[0]
        out = jnp.zeros((x.shape[0], 2 * rows, x.shape[2]), x.dtype)
        for half, base in zip(halves, bases):
            out = lax.dynamic_update_slice_in_dim(out, half, base, axis=1)
        return lax.psum(out, axis) * scale, late_fn(early)
    order = ring_order(n)
    chunk = rows // n
    plans = []
    for r, ring in enumerate((order, order[::-1])):
        pos_tab = np.zeros(n, np.int32)
        for i, dev in enumerate(ring):
            pos_tab[dev] = i
        p = jnp.asarray(pos_tab)[lax.axis_index(axis)]
        perm = [(ring[i], ring[(i + 1) % n]) for i in range(n)]
        plans.append((bases[r], p, perm))

    def piece(x, p, k):
        return lax.dynamic_slice_in_dim(x, ((p - k) % n) * chunk, chunk, axis=1)

    accs = [piece(x, p, 0) for x, (_, p, _) in zip(halves, plans)]
    for k in range(n - 1):
        if k == 1:
            accs, early = lax.optimization_barrier((accs, early))
            hold = late_fn(early)
        accs = [
            lax.ppermute(acc, axis, plan[2]) + piece(x, plan[1], k + 1)
            for acc, x, plan in zip(accs, halves, plans)
        ]
    accs = [acc * scale for acc in accs]
    x = halves[0]
    out = jnp.zeros((x.shape[0], 2 * rows, x.shape[2]), x.dtype)
    for acc, (base, p, _) in zip(accs, plans):
        out = lax.dynamic_update_slice_in_dim(out, acc, base + ((p + 1) % n) * chunk, axis=1)
    curs = accs
    for k in range(n - 1):
        curs = [lax.ppermute(cur, axis, plan[2]) for cur, plan in zip(curs, plans)]
        if k == n // 2:
            curs, hold = lax.optimization_barrier((curs, hold))
        for cur, (base, p, _) in zip(curs, plans):
            out = lax.dynamic_update_slice_in_dim(out, cur, base + ((p - k) % n) * chunk, axis=1)
    return out, hold


def shards(inputs, grad_out, weights):
    planes, ny, nz, fshare = grad_out.shape
    cin = weights.shape[3]
    voxels = planes * ny * nz
    scale = 1.0 / math.sqrt(voxels * lax.axis_size("space"))
    grad_rimmed = extended(grad_out, (("space", 0),), 1)
    grad_padded = jnp.pad(grad_rimmed, ((0, 0), (1, 1), (1, 1), (0, 0)))
    gathered = lax.all_gather(inputs, "filt", axis=3, tiled=True)
    width = gathered.shape[3]
    fsize = lax.axis_size("filt")
    f = lax.axis_index("filt")
    if fsize == 4:
        partner = lax.ppermute(inputs, "filt", [(i, i ^ 1) for i in range(fsize)])
        core, chip = f % 2, f // 2
        own_half = jnp.where(
            core == 0,
            jnp.concatenate([inputs, partner], axis=3),
            jnp.concatenate([partner, inputs], axis=3),
        )
        other_half = lax.dynamic_slice_in_dim(gathered, (1 - chip) * 2 * fshare, 2 * fshare, axis=3)
        bases = [chip * 2 * fshare, (1 - chip) * 2 * fshare]
    else:
        own_half = gathered[..., : width // 2]
        other_half = gathered[..., width // 2 :]
        bases = [0, width // 2]
    first = weight_taps(own_half.reshape(voxels, -1), grad_padded, 0, 1)
    first, other_half = lax.optimization_barrier((first, other_half))
    second = weight_taps(other_half.reshape(voxels, -1), grad_padded, 0, 1)
    def input_grad(early):
        grad_padded, weights = early
        data_term = jnp.zeros((voxels, cin), jnp.float32)
        for a in (1, 0, 2):
            moved_list = []
            for data_b in range(3):
                for data_c in range(3):
                    moved_list.append(
                        grad_padded[
                            2 - a : 2 - a + planes,
                            2 - data_b : 2 - data_b + ny,
                            2 - data_c : 2 - data_c + nz,
                            :,
                        ].reshape(voxels, fshare)
                    )
            stacked = jnp.stack(moved_list, axis=1).reshape(voxels, 3, 3, fshare)
            data_term = data_term + lax.dot_general(
                stacked,
                weights[a],
                (((1, 2, 3), (0, 1, 3)), ((), ())),
                preferred_element_type=jnp.float32,
            )
        return lax.psum_scatter(
            data_term.reshape(planes, ny, nz, cin), "filt", scatter_dimension=3, tiled=True
        ).astype(jnp.bfloat16)

    summed, grad_inputs = ring_sum(
        [first, second], bases, "space", scale, (grad_padded, weights), input_grad
    )
    weight_grad = summed.reshape(3, 3, 3, width, fshare)
    return (grad_inputs, weight_grad)


def solution(mesh):
    placed = (
        P("space", None, None, "filt"),
        P("space", None, None, "filt"),
        P(None, None, None, None, "filt"),
    )
    return jax.shard_map(
        shards,
        mesh=mesh,
        in_specs=placed,
        out_specs=(P("space", None, None, "filt"), P(None, None, None, None, "filt")),
        check_vma=False,
    )
```

```python
import math

import jax
import jax.numpy as jnp
import numpy as np
from jax import lax
from jax.experimental import pallas as pl
from jax.experimental.pallas import tpu as pltpu
from jax.sharding import PartitionSpec as P


def extended(array, sides, width):
    for axis, dim in sides:
        size, length = (lax.axis_size(axis), array.shape[dim])
        up = [(i, (i + 1) % size) for i in range(size - 1)]
        down = [(j, i) for i, j in up]
        last = lax.slice_in_dim(array, length - width, length, axis=dim)
        first = lax.slice_in_dim(array, 0, width, axis=dim)
        before = lax.ppermute(last, axis, up)
        after = lax.ppermute(first, axis, down)
        array = jnp.concatenate([before, array, after], axis=dim)
    return array


def wgrad_kernel(int_ref, g0_ref, g1_ref, g2_ref, out_ref):
    a = pl.program_id(0)
    b = pl.program_id(1)
    planes = g0_ref.shape[0] - 2
    ny = g0_ref.shape[1] - 2
    for c, g_ref in enumerate((g0_ref, g1_ref, g2_ref)):
        win = g_ref[pl.ds(2 - a, planes), pl.ds(2 - b, ny), :, :]
        moved = win.reshape(-1, win.shape[-1])
        out_ref[c] = lax.dot_general(
            int_ref[...], moved, (((0,), (0,)), ((), ())), preferred_element_type=jnp.float32
        )

def weight_taps(in_t, grad_padded, part, parts):
    planes2, ny2, nz2, fshare = grad_padded.shape
    nz = nz2 - 2
    voxels, width = in_t.shape
    width //= parts
    shifted = [grad_padded[:, :, 2 - c : 2 - c + nz, :] for c in range(3)]
    full = lambda shape: pl.BlockSpec(shape, lambda a, b: (0,) * len(shape))
    return pl.pallas_call(
        wgrad_kernel,
        grid=(3, 3),
        in_specs=[pl.BlockSpec((voxels, width), lambda a, b: (0, part))]
        + [full(s.shape) for s in shifted],
        out_specs=pl.BlockSpec((3, width, fshare), lambda a, b: (a * 3 + b, 0, 0)),
        out_shape=jax.ShapeDtypeStruct((27, width, fshare), jnp.float32),
        compiler_params=pltpu.CompilerParams(vmem_limit_bytes=48 * 1024 * 1024),
        cost_estimate=pl.CostEstimate(flops=2 * 27 * width * voxels * fshare, transcendentals=0,
                                      bytes_accessed=voxels * width * 2 + 3 * shifted[0].size * 2 + 27 * width * fshare * 4),
    )(in_t, *shifted)

def ring_order(n):
    if n % 2:
        return list(range(n))
    return list(range(0, n, 2)) + list(range(n - 1, 0, -2))


def ring_sum(halves, bases, axis, scale, early, late_fn):
    n = lax.axis_size(axis)
    rows = halves[0].shape[1]
    x = halves[0]
    out = jnp.zeros((x.shape[0], 2 * rows, x.shape[2]), x.dtype)
    if n == 1 or rows % (8 * n):
        for half, base in zip(halves, bases):
            out = lax.dynamic_update_slice_in_dim(out, half, base, axis=1)
        return lax.psum(out, axis) * scale, late_fn(early)
    order = ring_order(n)
    chunk = rows // n
    me = lax.axis_index(axis)
    plans = []
    for ring in (order, order[::-1]):
        pos_tab = np.zeros(n, np.int32)
        for i, dev in enumerate(ring):
            pos_tab[dev] = i
        p = jnp.asarray(pos_tab)[me]
        perm = [(ring[i], ring[(i + 1) % n]) for i in range(n)]
        owner = jnp.asarray(np.array([ring[(j - 1) % n] for j in range(n)], np.int32))
        plans.append((p, perm, owner))

    def piece(x, plan, k, relabel):
        p, _, owner = plan
        j = (p - k) % n
        start = owner[j] * chunk if relabel else j * chunk
        return lax.dynamic_slice_in_dim(x, start, chunk, axis=1)

    relabels = (False, True)
    accs = [piece(x, plan, 0, rl) for x, plan, rl in zip(halves, plans, relabels)]
    for k in range(n - 1):
        accs = [
            lax.ppermute(acc, axis, plan[1]) + piece(x, plan, k + 1, rl)
            for acc, x, plan, rl in zip(accs, halves, plans, relabels)
        ]
    accs = [acc * scale for acc in accs]
    accs, early = lax.optimization_barrier((accs, early))
    hold = late_fn(early)
    gathered = lax.all_gather(accs[1], axis, axis=1, tiled=True)
    out = lax.dynamic_update_slice_in_dim(out, gathered, bases[1], axis=1)
    p = plans[0][0]
    out = lax.dynamic_update_slice_in_dim(out, accs[0], bases[0] + ((p + 1) % n) * chunk, axis=1)
    cur = accs[0]
    for k in range(n - 1):
        cur = lax.ppermute(cur, axis, plans[0][1])
        out = lax.dynamic_update_slice_in_dim(out, cur, bases[0] + ((p - k) % n) * chunk, axis=1)
    return out, hold


def shards(inputs, grad_out, weights):
    planes, ny, nz, fshare = grad_out.shape
    cin = weights.shape[3]
    voxels = planes * ny * nz
    scale = 1.0 / math.sqrt(voxels * lax.axis_size("space"))
    grad_rimmed = extended(grad_out, (("space", 0),), 1)
    grad_padded = jnp.pad(grad_rimmed, ((0, 0), (1, 1), (1, 1), (0, 0)))
    gathered = lax.all_gather(inputs, "filt", axis=3, tiled=True)
    width = gathered.shape[3]
    fsize = lax.axis_size("filt")
    f = lax.axis_index("filt")
    if fsize == 4:
        partner = lax.ppermute(inputs, "filt", [(i, i ^ 1) for i in range(fsize)])
        core, chip = f % 2, f // 2
        own_half = jnp.where(
            core == 0,
            jnp.concatenate([inputs, partner], axis=3),
            jnp.concatenate([partner, inputs], axis=3),
        )
        other_half = lax.dynamic_slice_in_dim(gathered, (1 - chip) * 2 * fshare, 2 * fshare, axis=3)
        bases = [chip * 2 * fshare, (1 - chip) * 2 * fshare]
    else:
        own_half = gathered[..., : width // 2]
        other_half = gathered[..., width // 2 :]
        bases = [0, width // 2]
    first = weight_taps(own_half.reshape(voxels, -1), grad_padded, 0, 1)
    first, other_half = lax.optimization_barrier((first, other_half))
    second = weight_taps(other_half.reshape(voxels, -1), grad_padded, 0, 1)
    def input_grad(early):
        grad_padded, weights = early
        data_term = jnp.zeros((voxels, cin), jnp.float32)
        for a in (1, 0, 2):
            moved_list = []
            for data_b in range(3):
                for data_c in range(3):
                    moved_list.append(
                        grad_padded[
                            2 - a : 2 - a + planes,
                            2 - data_b : 2 - data_b + ny,
                            2 - data_c : 2 - data_c + nz,
                            :,
                        ].reshape(voxels, fshare)
                    )
            stacked = jnp.stack(moved_list, axis=1).reshape(voxels, 3, 3, fshare)
            data_term = data_term + lax.dot_general(
                stacked,
                weights[a],
                (((1, 2, 3), (0, 1, 3)), ((), ())),
                preferred_element_type=jnp.float32,
            )
        return lax.psum_scatter(
            data_term.reshape(planes, ny, nz, cin), "filt", scatter_dimension=3, tiled=True
        ).astype(jnp.bfloat16)

    summed, grad_inputs = ring_sum(
        [first, second], bases, "space", scale, (grad_padded, weights), input_grad
    )
    weight_grad = summed.reshape(3, 3, 3, width, fshare)
    return (grad_inputs, weight_grad)


def solution(mesh):
    placed = (
        P("space", None, None, "filt"),
        P("space", None, None, "filt"),
        P(None, None, None, None, "filt"),
    )
    return jax.shard_map(
        shards,
        mesh=mesh,
        in_specs=placed,
        out_specs=(P("space", None, None, "filt"), P(None, None, None, None, "filt")),
        check_vma=False,
    )
```

```python
import math

import jax
import jax.numpy as jnp
import numpy as np
from jax import lax
from jax.experimental import pallas as pl
from jax.experimental.pallas import tpu as pltpu
from jax.sharding import PartitionSpec as P


def extended(array, sides, width):
    for axis, dim in sides:
        size, length = (lax.axis_size(axis), array.shape[dim])
        up = [(i, (i + 1) % size) for i in range(size - 1)]
        down = [(j, i) for i, j in up]
        last = lax.slice_in_dim(array, length - width, length, axis=dim)
        first = lax.slice_in_dim(array, 0, width, axis=dim)
        before = lax.ppermute(last, axis, up)
        after = lax.ppermute(first, axis, down)
        array = jnp.concatenate([before, array, after], axis=dim)
    return array


def wgrad_kernel(int_ref, g0_ref, g1_ref, g2_ref, out_ref):
    a = pl.program_id(0)
    b = pl.program_id(1)
    planes = g0_ref.shape[0] - 2
    ny = g0_ref.shape[1] - 2
    fshare = g0_ref.shape[-1]
    moved = jnp.concatenate(
        [
            g_ref[pl.ds(2 - a, planes), pl.ds(2 - b, ny), :, :].reshape(-1, fshare)
            for g_ref in (g0_ref, g1_ref, g2_ref)
        ],
        axis=1,
    )
    res = lax.dot_general(
        int_ref[...], moved, (((0,), (0,)), ((), ())), preferred_element_type=jnp.float32
    )
    for c in range(3):
        out_ref[c] = res[:, c * fshare : (c + 1) * fshare]

def weight_taps(in_t, grad_padded, part, parts):
    planes2, ny2, nz2, fshare = grad_padded.shape
    nz = nz2 - 2
    voxels, width = in_t.shape
    width //= parts
    shifted = [grad_padded[:, :, 2 - c : 2 - c + nz, :] for c in range(3)]
    full = lambda shape: pl.BlockSpec(shape, lambda a, b: (0,) * len(shape))
    return pl.pallas_call(
        wgrad_kernel,
        grid=(3, 3),
        in_specs=[pl.BlockSpec((voxels, width), lambda a, b: (0, part))]
        + [full(s.shape) for s in shifted],
        out_specs=pl.BlockSpec((3, width, fshare), lambda a, b: (a * 3 + b, 0, 0)),
        out_shape=jax.ShapeDtypeStruct((27, width, fshare), jnp.float32),
        compiler_params=pltpu.CompilerParams(vmem_limit_bytes=48 * 1024 * 1024),
        cost_estimate=pl.CostEstimate(flops=2 * 27 * width * voxels * fshare, transcendentals=0,
                                      bytes_accessed=voxels * width * 2 + 3 * shifted[0].size * 2 + 27 * width * fshare * 4),
    )(in_t, *shifted)

def ring_order(n):
    if n % 2:
        return list(range(n))
    return list(range(0, n, 2)) + list(range(n - 1, 0, -2))


def ring_sum(halves, axis, scale, hold):
    n = lax.axis_size(axis)
    rows = halves[0].shape[1]
    if n == 1 or rows % (8 * n):
        return lax.psum(jnp.concatenate(halves, axis=1), axis) * scale, hold
    order = ring_order(n)
    chunk = rows // n
    plans = []
    for r, ring in enumerate((order, order[::-1])):
        pos_tab = np.zeros(n, np.int32)
        for i, dev in enumerate(ring):
            pos_tab[dev] = i
        p = jnp.asarray(pos_tab)[lax.axis_index(axis)]
        perm = [(ring[i], ring[(i + 1) % n]) for i in range(n)]
        plans.append((r * rows, p, perm))

    def piece(x, p, k):
        return lax.dynamic_slice_in_dim(x, ((p - k) % n) * chunk, chunk, axis=1)

    accs = []
    for x, (_, p, perm) in zip(halves, plans):
        acc = piece(x, p, 0)
        for k in range(n - 1):
            acc = lax.ppermute(acc, axis, perm) + piece(x, p, k + 1)
        accs.append(acc * scale)
    x = halves[0]
    out = jnp.zeros((x.shape[0], 2 * rows, x.shape[2]), x.dtype)
    for acc, (base, p, _) in zip(accs, plans):
        out = lax.dynamic_update_slice_in_dim(out, acc, base + ((p + 1) % n) * chunk, axis=1)
    curs = accs
    for k in range(n - 1):
        curs = [lax.ppermute(cur, axis, plan[2]) for cur, plan in zip(curs, plans)]
        if k == n // 2:
            curs, hold = lax.optimization_barrier((curs, hold))
        for cur, (base, p, _) in zip(curs, plans):
            out = lax.dynamic_update_slice_in_dim(out, cur, base + ((p - k) % n) * chunk, axis=1)
    return out, hold


def shards(inputs, grad_out, weights):
    planes, ny, nz, fshare = grad_out.shape
    cin = weights.shape[3]
    voxels = planes * ny * nz
    scale = 1.0 / math.sqrt(voxels * lax.axis_size("space"))
    grad_rimmed = extended(grad_out, (("space", 0),), 1)
    grad_padded = jnp.pad(grad_rimmed, ((0, 0), (1, 1), (1, 1), (0, 0)))
    gathered = lax.all_gather(inputs, "filt", axis=3, tiled=True)
    width = gathered.shape[3]
    data_term = jnp.zeros((voxels, cin), jnp.float32)
    for a in (1, 0, 2):
        moved_list = []
        for data_b in range(3):
            for data_c in range(3):
                moved_list.append(
                    grad_padded[
                        2 - a : 2 - a + planes,
                        2 - data_b : 2 - data_b + ny,
                        2 - data_c : 2 - data_c + nz,
                        :,
                    ].reshape(voxels, fshare)
                )
        stacked = jnp.stack(moved_list, axis=1).reshape(voxels, 3, 3, fshare)
        data_term = data_term + lax.dot_general(
            stacked,
            weights[a],
            (((1, 2, 3), (0, 1, 3)), ((), ())),
            preferred_element_type=jnp.float32,
        )
    data_term, gathered = lax.optimization_barrier((data_term, gathered))
    grad_inputs = lax.psum_scatter(
        data_term.reshape(planes, ny, nz, cin), "filt", scatter_dimension=3, tiled=True
    ).astype(jnp.bfloat16)
    in_t = gathered.reshape(voxels, width)
    halves = [weight_taps(in_t, grad_padded, 0, 2), weight_taps(in_t, grad_padded, 1, 2)]
    summed, grad_inputs = ring_sum(halves, "space", scale, grad_inputs)
    weight_grad = summed.reshape(3, 3, 3, width, fshare)
    return (grad_inputs, weight_grad)


def solution(mesh):
    placed = (
        P("space", None, None, "filt"),
        P("space", None, None, "filt"),
        P(None, None, None, None, "filt"),
    )
    return jax.shard_map(
        shards,
        mesh=mesh,
        in_specs=placed,
        out_specs=(P("space", None, None, "filt"), P(None, None, None, None, "filt")),
        check_vma=False,
    )
```

```python
import math

import jax
import jax.numpy as jnp
import numpy as np
from jax import lax
from jax.experimental import pallas as pl
from jax.experimental.pallas import tpu as pltpu
from jax.sharding import PartitionSpec as P


def extended(array, sides, width):
    for axis, dim in sides:
        size, length = (lax.axis_size(axis), array.shape[dim])
        up = [(i, (i + 1) % size) for i in range(size - 1)]
        down = [(j, i) for i, j in up]
        last = lax.slice_in_dim(array, length - width, length, axis=dim)
        first = lax.slice_in_dim(array, 0, width, axis=dim)
        before = lax.ppermute(last, axis, up)
        after = lax.ppermute(first, axis, down)
        array = jnp.concatenate([before, array, after], axis=dim)
    return array


def wgrad_kernel(int_ref, g0_ref, g1_ref, g2_ref, out_ref):
    a = pl.program_id(0)
    planes = g0_ref.shape[0] - 2
    ny = g0_ref.shape[1] - 2
    fshare = g0_ref.shape[-1]
    moved = jnp.concatenate(
        [
            g_ref[pl.ds(2 - a, planes), 2 - b : 2 - b + ny, :, :].reshape(-1, fshare)
            for b in range(3)
            for g_ref in (g0_ref, g1_ref, g2_ref)
        ],
        axis=1,
    )
    res = lax.dot_general(
        int_ref[...], moved, (((0,), (0,)), ((), ())), preferred_element_type=jnp.float32
    )
    for t in range(9):
        out_ref[t] = res[:, t * fshare : (t + 1) * fshare]


def weight_taps(in_t, grad_padded, part, parts):
    planes2, ny2, nz2, fshare = grad_padded.shape
    nz = nz2 - 2
    voxels, width = in_t.shape
    width //= parts
    shifted = [grad_padded[:, :, 2 - c : 2 - c + nz, :] for c in range(3)]
    full = lambda shape: pl.BlockSpec(shape, lambda a: (0,) * len(shape))
    return pl.pallas_call(
        wgrad_kernel,
        grid=(3,),
        in_specs=[pl.BlockSpec((voxels, width), lambda a: (0, part))]
        + [full(s.shape) for s in shifted],
        out_specs=pl.BlockSpec((9, width, fshare), lambda a: (a, 0, 0)),
        out_shape=jax.ShapeDtypeStruct((27, width, fshare), jnp.float32),
        compiler_params=pltpu.CompilerParams(vmem_limit_bytes=48 * 1024 * 1024),
        cost_estimate=pl.CostEstimate(flops=2 * 27 * width * voxels * fshare, transcendentals=0,
                                      bytes_accessed=voxels * width * 2 + 3 * shifted[0].size * 2 + 27 * width * fshare * 4),
    )(in_t, *shifted)


def ring_order(n):
    if n % 2:
        return list(range(n))
    return list(range(0, n, 2)) + list(range(n - 1, 0, -2))


def ring_sum(halves, axis, scale, hold):
    n = lax.axis_size(axis)
    rows = halves[0].shape[1]
    if n == 1 or rows % (8 * n):
        return lax.psum(jnp.concatenate(halves, axis=1), axis) * scale, hold
    order = ring_order(n)
    chunk = rows // n
    plans = []
    for r, ring in enumerate((order, order[::-1])):
        pos_tab = np.zeros(n, np.int32)
        for i, dev in enumerate(ring):
            pos_tab[dev] = i
        p = jnp.asarray(pos_tab)[lax.axis_index(axis)]
        perm = [(ring[i], ring[(i + 1) % n]) for i in range(n)]
        plans.append((r * rows, p, perm))

    def piece(x, p, k):
        return lax.dynamic_slice_in_dim(x, ((p - k) % n) * chunk, chunk, axis=1)

    accs = []
    for x, (_, p, perm) in zip(halves, plans):
        acc = piece(x, p, 0)
        for k in range(n - 1):
            acc = lax.ppermute(acc, axis, perm) + piece(x, p, k + 1)
        accs.append(acc * scale)
    x = halves[0]
    out = jnp.zeros((x.shape[0], 2 * rows, x.shape[2]), x.dtype)
    for acc, (base, p, _) in zip(accs, plans):
        out = lax.dynamic_update_slice_in_dim(out, acc, base + ((p + 1) % n) * chunk, axis=1)
    curs = accs
    for k in range(n - 1):
        curs = [lax.ppermute(cur, axis, plan[2]) for cur, plan in zip(curs, plans)]
        if k == n // 2:
            curs, hold = lax.optimization_barrier((curs, hold))
        for cur, (base, p, _) in zip(curs, plans):
            out = lax.dynamic_update_slice_in_dim(out, cur, base + ((p - k) % n) * chunk, axis=1)
    return out, hold


def shards(inputs, grad_out, weights):
    planes, ny, nz, fshare = grad_out.shape
    cin = weights.shape[3]
    voxels = planes * ny * nz
    scale = 1.0 / math.sqrt(voxels * lax.axis_size("space"))
    grad_rimmed = extended(grad_out, (("space", 0),), 1)
    grad_padded = jnp.pad(grad_rimmed, ((0, 0), (1, 1), (1, 1), (0, 0)))
    gathered = lax.all_gather(inputs, "filt", axis=3, tiled=True)
    width = gathered.shape[3]
    data_term = jnp.zeros((voxels, cin), jnp.float32)
    for a in (1, 0, 2):
        moved_list = []
        for data_b in range(3):
            for data_c in range(3):
                moved_list.append(
                    grad_padded[
                        2 - a : 2 - a + planes,
                        2 - data_b : 2 - data_b + ny,
                        2 - data_c : 2 - data_c + nz,
                        :,
                    ].reshape(voxels, fshare)
                )
        stacked = jnp.stack(moved_list, axis=1).reshape(voxels, 3, 3, fshare)
        data_term = data_term + lax.dot_general(
            stacked,
            weights[a],
            (((1, 2, 3), (0, 1, 3)), ((), ())),
            preferred_element_type=jnp.float32,
        )
    data_term, gathered = lax.optimization_barrier((data_term, gathered))
    grad_inputs = lax.psum_scatter(
        data_term.reshape(planes, ny, nz, cin), "filt", scatter_dimension=3, tiled=True
    ).astype(jnp.bfloat16)
    in_t = gathered.reshape(voxels, width)
    halves = [weight_taps(in_t, grad_padded, 0, 2), weight_taps(in_t, grad_padded, 1, 2)]
    summed, grad_inputs = ring_sum(halves, "space", scale, grad_inputs)
    weight_grad = summed.reshape(3, 3, 3, width, fshare)
    return (grad_inputs, weight_grad)


def solution(mesh):
    placed = (
        P("space", None, None, "filt"),
        P("space", None, None, "filt"),
        P(None, None, None, None, "filt"),
    )
    return jax.shard_map(
        shards,
        mesh=mesh,
        in_specs=placed,
        out_specs=(P("space", None, None, "filt"), P(None, None, None, None, "filt")),
        check_vma=False,
    )
```

```python
import math

import jax
import jax.numpy as jnp
import numpy as np
from jax import lax
from jax.experimental import pallas as pl
from jax.experimental.pallas import tpu as pltpu
from jax.sharding import PartitionSpec as P


def extended(array, sides, width):
    for axis, dim in sides:
        size, length = (lax.axis_size(axis), array.shape[dim])
        up = [(i, (i + 1) % size) for i in range(size - 1)]
        down = [(j, i) for i, j in up]
        last = lax.slice_in_dim(array, length - width, length, axis=dim)
        first = lax.slice_in_dim(array, 0, width, axis=dim)
        before = lax.ppermute(last, axis, up)
        after = lax.ppermute(first, axis, down)
        array = jnp.concatenate([before, array, after], axis=dim)
    return array


def wgrad_kernel(int_ref, g0_ref, g1_ref, g2_ref, out_ref):
    a = pl.program_id(0)
    planes = g0_ref.shape[0] - 2
    ny = g0_ref.shape[1] - 2
    fshare = g0_ref.shape[-1]
    moved = jnp.concatenate(
        [
            g_ref[pl.ds(2 - a, planes), 2 - b : 2 - b + ny, :, :].reshape(-1, fshare)
            for b in range(3)
            for g_ref in (g0_ref, g1_ref, g2_ref)
        ],
        axis=1,
    )
    res = lax.dot_general(
        int_ref[...], moved, (((0,), (0,)), ((), ())), preferred_element_type=jnp.float32
    )
    for t in range(9):
        out_ref[t] = res[:, t * fshare : (t + 1) * fshare]


def weight_taps(in_t, grad_padded, part, parts):
    planes2, ny2, nz2, fshare = grad_padded.shape
    nz = nz2 - 2
    voxels, width = in_t.shape
    width //= parts
    shifted = [grad_padded[:, :, 2 - c : 2 - c + nz, :] for c in range(3)]
    full = lambda shape: pl.BlockSpec(shape, lambda a: (0,) * len(shape))
    return pl.pallas_call(
        wgrad_kernel,
        grid=(3,),
        in_specs=[pl.BlockSpec((voxels, width), lambda a: (0, part))]
        + [full(s.shape) for s in shifted],
        out_specs=pl.BlockSpec((9, width, fshare), lambda a: (a, 0, 0)),
        out_shape=jax.ShapeDtypeStruct((27, width, fshare), jnp.float32),
        compiler_params=pltpu.CompilerParams(vmem_limit_bytes=48 * 1024 * 1024),
        cost_estimate=pl.CostEstimate(flops=2 * 27 * width * voxels * fshare, transcendentals=0,
                                      bytes_accessed=voxels * width * 2 + 3 * shifted[0].size * 2 + 27 * width * fshare * 4),
    )(in_t, *shifted)


def ring_order(n):
    if n % 2:
        return list(range(n))
    return list(range(0, n, 2)) + list(range(n - 1, 0, -2))


def ring_sum(halves, bases, axis, scale, hold):
    n = lax.axis_size(axis)
    rows = halves[0].shape[1]
    if n == 1 or rows % (8 * n):
        x = halves[0]
        out = jnp.zeros((x.shape[0], 2 * rows, x.shape[2]), x.dtype)
        for half, base in zip(halves, bases):
            out = lax.dynamic_update_slice_in_dim(out, half, base, axis=1)
        return lax.psum(out, axis) * scale, hold
    order = ring_order(n)
    chunk = rows // n
    plans = []
    for r, ring in enumerate((order, order[::-1])):
        pos_tab = np.zeros(n, np.int32)
        for i, dev in enumerate(ring):
            pos_tab[dev] = i
        p = jnp.asarray(pos_tab)[lax.axis_index(axis)]
        perm = [(ring[i], ring[(i + 1) % n]) for i in range(n)]
        plans.append((bases[r], p, perm))

    def piece(x, p, k):
        return lax.dynamic_slice_in_dim(x, ((p - k) % n) * chunk, chunk, axis=1)

    accs = []
    for x, (_, p, perm) in zip(halves, plans):
        acc = piece(x, p, 0)
        for k in range(n - 1):
            acc = lax.ppermute(acc, axis, perm) + piece(x, p, k + 1)
        accs.append(acc * scale)
    x = halves[0]
    out = jnp.zeros((x.shape[0], 2 * rows, x.shape[2]), x.dtype)
    for acc, (base, p, _) in zip(accs, plans):
        out = lax.dynamic_update_slice_in_dim(out, acc, base + ((p + 1) % n) * chunk, axis=1)
    curs = accs
    for k in range(n - 1):
        curs = [lax.ppermute(cur, axis, plan[2]) for cur, plan in zip(curs, plans)]
        if k == n // 2:
            curs, hold = lax.optimization_barrier((curs, hold))
        for cur, (base, p, _) in zip(curs, plans):
            out = lax.dynamic_update_slice_in_dim(out, cur, base + ((p - k) % n) * chunk, axis=1)
    return out, hold


def shards(inputs, grad_out, weights):
    planes, ny, nz, fshare = grad_out.shape
    cin = weights.shape[3]
    voxels = planes * ny * nz
    scale = 1.0 / math.sqrt(voxels * lax.axis_size("space"))
    grad_rimmed = extended(grad_out, (("space", 0),), 1)
    grad_padded = jnp.pad(grad_rimmed, ((0, 0), (1, 1), (1, 1), (0, 0)))
    gathered = lax.all_gather(inputs, "filt", axis=3, tiled=True)
    width = gathered.shape[3]
    data_term = jnp.zeros((voxels, cin), jnp.float32)
    for a in (1, 0, 2):
        moved_list = []
        for data_b in range(3):
            for data_c in range(3):
                moved_list.append(
                    grad_padded[
                        2 - a : 2 - a + planes,
                        2 - data_b : 2 - data_b + ny,
                        2 - data_c : 2 - data_c + nz,
                        :,
                    ].reshape(voxels, fshare)
                )
        stacked = jnp.stack(moved_list, axis=1).reshape(voxels, 3, 3, fshare)
        data_term = data_term + lax.dot_general(
            stacked,
            weights[a],
            (((1, 2, 3), (0, 1, 3)), ((), ())),
            preferred_element_type=jnp.float32,
        )
    fsplit = lax.axis_size("filt") == 4
    own_half = None
    if fsplit:
        f = lax.axis_index("filt")
        partner = lax.ppermute(inputs, "filt", [(i, i ^ 1) for i in range(4)])
        own_half = jnp.where(
            f % 2 == 0,
            jnp.concatenate([inputs, partner], axis=3),
            jnp.concatenate([partner, inputs], axis=3),
        )
    data_term, gathered, own_half = lax.optimization_barrier((data_term, gathered, own_half))
    grad_inputs = lax.psum_scatter(
        data_term.reshape(planes, ny, nz, cin), "filt", scatter_dimension=3, tiled=True
    ).astype(jnp.bfloat16)
    in_t = gathered.reshape(voxels, width)
    if fsplit:
        f = lax.axis_index("filt")
        first = weight_taps(own_half.reshape(voxels, width // 2), grad_padded, 0, 1)
        first, in_t = lax.optimization_barrier((first, in_t))
        other_half = lax.dynamic_slice_in_dim(in_t, (1 - f // 2) * (width // 2), width // 2, axis=1)
        second = weight_taps(other_half, grad_padded, 0, 1)
        bases = [(f // 2) * (width // 2), (1 - f // 2) * (width // 2)]
    else:
        first = weight_taps(in_t, grad_padded, 0, 2)
        second = weight_taps(in_t, grad_padded, 1, 2)
        bases = [0, width // 2]
    summed, grad_inputs = ring_sum([first, second], bases, "space", scale, grad_inputs)
    weight_grad = summed.reshape(3, 3, 3, width, fshare)
    return (grad_inputs, weight_grad)


def solution(mesh):
    placed = (
        P("space", None, None, "filt"),
        P("space", None, None, "filt"),
        P(None, None, None, None, "filt"),
    )
    return jax.shard_map(
        shards,
        mesh=mesh,
        in_specs=placed,
        out_specs=(P("space", None, None, "filt"), P(None, None, None, None, "filt")),
        check_vma=False,
    )
```

```python
import math

import jax
import jax.numpy as jnp
import numpy as np
from jax import lax
from jax.experimental import pallas as pl
from jax.experimental.pallas import tpu as pltpu
from jax.sharding import PartitionSpec as P


def extended(array, sides, width):
    for axis, dim in sides:
        size, length = (lax.axis_size(axis), array.shape[dim])
        up = [(i, (i + 1) % size) for i in range(size - 1)]
        down = [(j, i) for i, j in up]
        last = lax.slice_in_dim(array, length - width, length, axis=dim)
        first = lax.slice_in_dim(array, 0, width, axis=dim)
        before = lax.ppermute(last, axis, up)
        after = lax.ppermute(first, axis, down)
        array = jnp.concatenate([before, array, after], axis=dim)
    return array


def wgrad_kernel(int_ref, g0_ref, g1_ref, g2_ref, out_ref):
    a = pl.program_id(0)
    planes = g0_ref.shape[0] - 2
    ny = g0_ref.shape[1] - 2
    fshare = g0_ref.shape[-1]
    moved = jnp.concatenate(
        [
            g_ref[pl.ds(2 - a, planes), 2 - b : 2 - b + ny, :, :].reshape(-1, fshare)
            for b in range(3)
            for g_ref in (g0_ref, g1_ref, g2_ref)
        ],
        axis=1,
    )
    res = lax.dot_general(
        int_ref[...], moved, (((0,), (0,)), ((), ())), preferred_element_type=jnp.float32
    )
    out_ref[...] = res


def weight_taps(in_t, grad_padded, part, parts):
    planes2, ny2, nz2, fshare = grad_padded.shape
    nz = nz2 - 2
    voxels, width = in_t.shape
    width //= parts
    shifted = [grad_padded[:, :, 2 - c : 2 - c + nz, :] for c in range(3)]
    full = lambda shape: pl.BlockSpec(shape, lambda a: (0,) * len(shape))
    return pl.pallas_call(
        wgrad_kernel,
        grid=(3,),
        in_specs=[pl.BlockSpec((voxels, width), lambda a: (0, part))]
        + [full(s.shape) for s in shifted],
        out_specs=pl.BlockSpec((width, 9 * fshare), lambda a: (0, a)),
        out_shape=jax.ShapeDtypeStruct((width, 27 * fshare), jnp.float32),
        compiler_params=pltpu.CompilerParams(vmem_limit_bytes=48 * 1024 * 1024),
        cost_estimate=pl.CostEstimate(flops=2 * 27 * width * voxels * fshare, transcendentals=0,
                                      bytes_accessed=voxels * width * 2 + 3 * shifted[0].size * 2 + 27 * width * fshare * 4),
    )(in_t, *shifted)


def ring_order(n):
    if n % 2:
        return list(range(n))
    return list(range(0, n, 2)) + list(range(n - 1, 0, -2))


def ring_sum(halves, bases, axis, scale, hold, cout):
    n = lax.axis_size(axis)
    rows = halves[0].shape[0]
    taps = halves[0].shape[1] // cout

    def tap_major(block):
        return block.reshape(block.shape[0], taps, cout).transpose(1, 0, 2)

    out = jnp.zeros((taps, 2 * rows, cout), halves[0].dtype)
    if n == 1 or rows % (8 * n):
        for half, base in zip(halves, bases):
            out = lax.dynamic_update_slice_in_dim(out, tap_major(half), base, axis=1)
        return lax.psum(out, axis) * scale, hold
    order = ring_order(n)
    chunk = rows // n
    plans = []
    for r, ring in enumerate((order, order[::-1])):
        pos_tab = np.zeros(n, np.int32)
        for i, dev in enumerate(ring):
            pos_tab[dev] = i
        p = jnp.asarray(pos_tab)[lax.axis_index(axis)]
        perm = [(ring[i], ring[(i + 1) % n]) for i in range(n)]
        plans.append((bases[r], p, perm))

    def piece(x, p, k):
        return lax.dynamic_slice_in_dim(x, ((p - k) % n) * chunk, chunk, axis=0)

    accs = []
    for x, (_, p, perm) in zip(halves, plans):
        acc = piece(x, p, 0)
        for k in range(n - 1):
            acc = lax.ppermute(acc, axis, perm) + piece(x, p, k + 1)
        accs.append(acc * scale)
    for acc, (base, p, _) in zip(accs, plans):
        out = lax.dynamic_update_slice_in_dim(out, tap_major(acc), base + ((p + 1) % n) * chunk, axis=1)
    curs = accs
    for k in range(n - 1):
        curs = [lax.ppermute(cur, axis, plan[2]) for cur, plan in zip(curs, plans)]
        if k == n // 2:
            curs, hold = lax.optimization_barrier((curs, hold))
        for cur, (base, p, _) in zip(curs, plans):
            out = lax.dynamic_update_slice_in_dim(out, tap_major(cur), base + ((p - k) % n) * chunk, axis=1)
    return out, hold


def shards(inputs, grad_out, weights):
    planes, ny, nz, fshare = grad_out.shape
    cin = weights.shape[3]
    voxels = planes * ny * nz
    scale = 1.0 / math.sqrt(voxels * lax.axis_size("space"))
    grad_rimmed = extended(grad_out, (("space", 0),), 1)
    grad_padded = jnp.pad(grad_rimmed, ((0, 0), (1, 1), (1, 1), (0, 0)))
    gathered = lax.all_gather(inputs, "filt", axis=3, tiled=True)
    width = gathered.shape[3]
    data_term = jnp.zeros((voxels, cin), jnp.float32)
    for a in (1, 0, 2):
        moved_list = []
        for data_b in range(3):
            for data_c in range(3):
                moved_list.append(
                    grad_padded[
                        2 - a : 2 - a + planes,
                        2 - data_b : 2 - data_b + ny,
                        2 - data_c : 2 - data_c + nz,
                        :,
                    ].reshape(voxels, fshare)
                )
        stacked = jnp.stack(moved_list, axis=1).reshape(voxels, 3, 3, fshare)
        data_term = data_term + lax.dot_general(
            stacked,
            weights[a],
            (((1, 2, 3), (0, 1, 3)), ((), ())),
            preferred_element_type=jnp.float32,
        )
    fsplit = lax.axis_size("filt") == 4
    own_half = None
    if fsplit:
        f = lax.axis_index("filt")
        partner = lax.ppermute(inputs, "filt", [(i, i ^ 1) for i in range(4)])
        own_half = jnp.where(
            f % 2 == 0,
            jnp.concatenate([inputs, partner], axis=3),
            jnp.concatenate([partner, inputs], axis=3),
        )
    data_term, gathered, own_half = lax.optimization_barrier((data_term, gathered, own_half))
    grad_inputs = lax.psum_scatter(
        data_term.reshape(planes, ny, nz, cin), "filt", scatter_dimension=3, tiled=True
    ).astype(jnp.bfloat16)
    in_t = gathered.reshape(voxels, width)
    if fsplit:
        f = lax.axis_index("filt")
        first = weight_taps(own_half.reshape(voxels, width // 2), grad_padded, 0, 1)
        first, in_t = lax.optimization_barrier((first, in_t))
        other_half = lax.dynamic_slice_in_dim(in_t, (1 - f // 2) * (width // 2), width // 2, axis=1)
        second = weight_taps(other_half, grad_padded, 0, 1)
        bases = [(f // 2) * (width // 2), (1 - f // 2) * (width // 2)]
    else:
        first = weight_taps(in_t, grad_padded, 0, 2)
        second = weight_taps(in_t, grad_padded, 1, 2)
        bases = [0, width // 2]
    summed, grad_inputs = ring_sum([first, second], bases, "space", scale, grad_inputs, fshare)
    weight_grad = summed.reshape(3, 3, 3, width, fshare)
    return (grad_inputs, weight_grad)


def solution(mesh):
    placed = (
        P("space", None, None, "filt"),
        P("space", None, None, "filt"),
        P(None, None, None, None, "filt"),
    )
    return jax.shard_map(
        shards,
        mesh=mesh,
        in_specs=placed,
        out_specs=(P("space", None, None, "filt"), P(None, None, None, None, "filt")),
        check_vma=False,
    )
```

```python
import math

import jax
import jax.numpy as jnp
import numpy as np
from jax import lax
from jax.experimental import pallas as pl
from jax.experimental.pallas import tpu as pltpu
from jax.sharding import PartitionSpec as P


def extended(array, sides, width):
    for axis, dim in sides:
        size, length = (lax.axis_size(axis), array.shape[dim])
        up = [(i, (i + 1) % size) for i in range(size - 1)]
        down = [(j, i) for i, j in up]
        last = lax.slice_in_dim(array, length - width, length, axis=dim)
        first = lax.slice_in_dim(array, 0, width, axis=dim)
        before = lax.ppermute(last, axis, up)
        after = lax.ppermute(first, axis, down)
        array = jnp.concatenate([before, array, after], axis=dim)
    return array


def wgrad_kernel(int_ref, g0_ref, g1_ref, g2_ref, out_ref):
    a = pl.program_id(0)
    planes = g0_ref.shape[0] - 2
    ny = g0_ref.shape[1] - 2
    fshare = g0_ref.shape[-1]
    moved = jnp.concatenate(
        [
            g_ref[pl.ds(2 - a, planes), 2 - b : 2 - b + ny, :, :].reshape(-1, fshare)
            for b in range(3)
            for g_ref in (g0_ref, g1_ref, g2_ref)
        ],
        axis=1,
    )
    res = lax.dot_general(
        int_ref[...], moved, (((0,), (0,)), ((), ())), preferred_element_type=jnp.float32
    )
    for t in range(9):
        out_ref[t] = res[:, t * fshare : (t + 1) * fshare]


def weight_taps(in_t, grad_padded, part, parts):
    planes2, ny2, nz2, fshare = grad_padded.shape
    nz = nz2 - 2
    voxels, width = in_t.shape
    width //= parts
    shifted = [grad_padded[:, :, 2 - c : 2 - c + nz, :] for c in range(3)]
    full = lambda shape: pl.BlockSpec(shape, lambda a: (0,) * len(shape))
    return pl.pallas_call(
        wgrad_kernel,
        grid=(3,),
        in_specs=[pl.BlockSpec((voxels, width), lambda a: (0, part))]
        + [full(s.shape) for s in shifted],
        out_specs=pl.BlockSpec((9, width, fshare), lambda a: (a, 0, 0)),
        out_shape=jax.ShapeDtypeStruct((27, width, fshare), jnp.float32),
        compiler_params=pltpu.CompilerParams(vmem_limit_bytes=48 * 1024 * 1024),
        cost_estimate=pl.CostEstimate(flops=2 * 27 * width * voxels * fshare, transcendentals=0,
                                      bytes_accessed=voxels * width * 2 + 3 * shifted[0].size * 2 + 27 * width * fshare * 4),
    )(in_t, *shifted)


def ring_order(n):
    if n % 2:
        return list(range(n))
    return list(range(0, n, 2)) + list(range(n - 1, 0, -2))


def ring_sum(halves, bases, axis, scale, hold):
    n = lax.axis_size(axis)
    rows = halves[0].shape[1]
    if n == 1 or rows % (8 * n):
        x = halves[0]
        out = jnp.zeros((x.shape[0], 2 * rows, x.shape[2]), x.dtype)
        for half, base in zip(halves, bases):
            out = lax.dynamic_update_slice_in_dim(out, half, base, axis=1)
        return lax.psum(out, axis) * scale, hold
    order = ring_order(n)
    chunk = rows // n
    plans = []
    for r, ring in enumerate((order, order[::-1])):
        pos_tab = np.zeros(n, np.int32)
        for i, dev in enumerate(ring):
            pos_tab[dev] = i
        p = jnp.asarray(pos_tab)[lax.axis_index(axis)]
        perm = [(ring[i], ring[(i + 1) % n]) for i in range(n)]
        plans.append((bases[r], p, perm))

    def piece(x, p, k):
        return lax.dynamic_slice_in_dim(x, ((p - k) % n) * chunk, chunk, axis=1)

    accs = []
    for x, (_, p, perm) in zip(halves, plans):
        acc = piece(x, p, 0)
        for k in range(n - 1):
            acc = lax.ppermute(acc, axis, perm) + piece(x, p, k + 1)
        accs.append(acc * scale)
    x = halves[0]
    out = jnp.zeros((x.shape[0], 2 * rows, x.shape[2]), x.dtype)
    for acc, (base, p, _) in zip(accs, plans):
        out = lax.dynamic_update_slice_in_dim(out, acc, base + ((p + 1) % n) * chunk, axis=1)
    curs = accs
    for k in range(n - 1):
        curs = [lax.ppermute(cur, axis, plan[2]) for cur, plan in zip(curs, plans)]
        if k == n // 2:
            curs, hold = lax.optimization_barrier((curs, hold))
        for cur, (base, p, _) in zip(curs, plans):
            out = lax.dynamic_update_slice_in_dim(out, cur, base + ((p - k) % n) * chunk, axis=1)
    return out, hold


def shards(inputs, grad_out, weights):
    planes, ny, nz, fshare = grad_out.shape
    cin = weights.shape[3]
    voxels = planes * ny * nz
    scale = 1.0 / math.sqrt(voxels * lax.axis_size("space"))
    grad_rimmed = extended(grad_out, (("space", 0),), 1)
    grad_padded = jnp.pad(grad_rimmed, ((0, 0), (1, 1), (1, 1), (0, 0)))
    gathered = lax.all_gather(inputs, "filt", axis=3, tiled=True)
    width = gathered.shape[3]
    data_term = jnp.zeros((voxels, cin), jnp.float32)
    for a in (1, 0, 2):
        moved_list = []
        for data_b in range(3):
            for data_c in range(3):
                moved_list.append(
                    grad_padded[
                        2 - a : 2 - a + planes,
                        2 - data_b : 2 - data_b + ny,
                        2 - data_c : 2 - data_c + nz,
                        :,
                    ].reshape(voxels, fshare)
                )
        stacked = jnp.stack(moved_list, axis=1).reshape(voxels, 3, 3, fshare)
        data_term = data_term + lax.dot_general(
            stacked,
            weights[a],
            (((1, 2, 3), (0, 1, 3)), ((), ())),
            preferred_element_type=jnp.float32,
        )
    fsplit = lax.axis_size("filt") == 4
    own_half = None
    if fsplit:
        f = lax.axis_index("filt")
        partner = lax.ppermute(inputs, "filt", [(i, i ^ 1) for i in range(4)])
        own_half = jnp.where(
            f % 2 == 0,
            jnp.concatenate([inputs, partner], axis=3),
            jnp.concatenate([partner, inputs], axis=3),
        )
    data_term, gathered, own_half = lax.optimization_barrier((data_term, gathered, own_half))
    grad_inputs = lax.psum_scatter(
        data_term.reshape(planes, ny, nz, cin), "filt", scatter_dimension=3, tiled=True
    ).astype(jnp.bfloat16)
    in_t = gathered.reshape(voxels, width)
    if fsplit:
        f = lax.axis_index("filt")
        first = weight_taps(own_half.reshape(voxels, width // 2), grad_padded, 0, 1)
        first, in_t = lax.optimization_barrier((first, in_t))
        other_half = lax.dynamic_slice_in_dim(in_t, (1 - f // 2) * (width // 2), width // 2, axis=1)
        second = weight_taps(other_half, grad_padded, 0, 1)
        bases = [(f // 2) * (width // 2), (1 - f // 2) * (width // 2)]
    else:
        first = weight_taps(in_t, grad_padded, 0, 2)
        second = weight_taps(in_t, grad_padded, 1, 2)
        bases = [0, width // 2]
    first, second = lax.optimization_barrier((first, second))
    summed, grad_inputs = ring_sum([first, second], bases, "space", scale, grad_inputs)
    weight_grad = summed.reshape(3, 3, 3, width, fshare)
    return (grad_inputs, weight_grad)


def solution(mesh):
    placed = (
        P("space", None, None, "filt"),
        P("space", None, None, "filt"),
        P(None, None, None, None, "filt"),
    )
    return jax.shard_map(
        shards,
        mesh=mesh,
        in_specs=placed,
        out_specs=(P("space", None, None, "filt"), P(None, None, None, None, "filt")),
        check_vma=False,
    )
```

```python
import math

import jax
import jax.numpy as jnp
import numpy as np
from jax import lax
from jax.experimental import pallas as pl
from jax.experimental.pallas import tpu as pltpu
from jax.sharding import PartitionSpec as P


def extended(array, sides, width):
    for axis, dim in sides:
        size, length = (lax.axis_size(axis), array.shape[dim])
        up = [(i, (i + 1) % size) for i in range(size - 1)]
        down = [(j, i) for i, j in up]
        last = lax.slice_in_dim(array, length - width, length, axis=dim)
        first = lax.slice_in_dim(array, 0, width, axis=dim)
        before = lax.ppermute(last, axis, up)
        after = lax.ppermute(first, axis, down)
        array = jnp.concatenate([before, array, after], axis=dim)
    return array


def wgrad_kernel(int_ref, g0_ref, g1_ref, g2_ref, out_ref):
    a = pl.program_id(0)
    planes = g0_ref.shape[0] - 2
    ny = g0_ref.shape[1] - 2
    fshare = g0_ref.shape[-1]
    moved = jnp.concatenate(
        [
            g_ref[pl.ds(2 - a, planes), 2 - b : 2 - b + ny, :, :].reshape(-1, fshare)
            for b in range(3)
            for g_ref in (g0_ref, g1_ref, g2_ref)
        ],
        axis=1,
    )
    res = lax.dot_general(
        int_ref[...], moved, (((0,), (0,)), ((), ())), preferred_element_type=jnp.float32
    )
    for t in range(9):
        out_ref[t] = res[:, t * fshare : (t + 1) * fshare]


def weight_taps(in_t, grad_padded, part, parts):
    planes2, ny2, nz2, fshare = grad_padded.shape
    nz = nz2 - 2
    voxels, width = in_t.shape
    width //= parts
    shifted = [grad_padded[:, :, 2 - c : 2 - c + nz, :] for c in range(3)]
    full = lambda shape: pl.BlockSpec(shape, lambda a: (0,) * len(shape))
    return pl.pallas_call(
        wgrad_kernel,
        grid=(3,),
        in_specs=[pl.BlockSpec((voxels, width), lambda a: (0, part))]
        + [full(s.shape) for s in shifted],
        out_specs=pl.BlockSpec((9, width, fshare), lambda a: (a, 0, 0)),
        out_shape=jax.ShapeDtypeStruct((27, width, fshare), jnp.float32),
        compiler_params=pltpu.CompilerParams(vmem_limit_bytes=48 * 1024 * 1024),
        cost_estimate=pl.CostEstimate(flops=2 * 27 * width * voxels * fshare, transcendentals=0,
                                      bytes_accessed=voxels * width * 2 + 3 * shifted[0].size * 2 + 27 * width * fshare * 4),
    )(in_t, *shifted)


def ring_order(n):
    if n % 2:
        return list(range(n))
    return list(range(0, n, 2)) + list(range(n - 1, 0, -2))


def ring_sum(halves, bases, axis, scale, hold):
    n = lax.axis_size(axis)
    rows = halves[0].shape[1]
    if n == 1 or rows % (8 * n):
        x = halves[0]
        out = jnp.zeros((x.shape[0], 2 * rows, x.shape[2]), x.dtype)
        for half, base in zip(halves, bases):
            out = lax.dynamic_update_slice_in_dim(out, half, base, axis=1)
        return lax.psum(out, axis) * scale, hold
    order = ring_order(n)
    chunk = rows // n
    plans = []
    for r, ring in enumerate((order, order[::-1])):
        pos_tab = np.zeros(n, np.int32)
        for i, dev in enumerate(ring):
            pos_tab[dev] = i
        p = jnp.asarray(pos_tab)[lax.axis_index(axis)]
        perm = [(ring[i], ring[(i + 1) % n]) for i in range(n)]
        plans.append((bases[r], p, perm))

    def piece(x, p, k):
        return lax.dynamic_slice_in_dim(x, ((p - k) % n) * chunk, chunk, axis=1)

    accs = []
    for x, (_, p, perm) in zip(halves, plans):
        acc = piece(x, p, 0)
        for k in range(n - 1):
            acc = lax.ppermute(acc, axis, perm) + piece(x, p, k + 1)
        accs.append(acc * scale)
    x = halves[0]
    out = jnp.zeros((x.shape[0], 2 * rows, x.shape[2]), x.dtype)
    for acc, (base, p, _) in zip(accs, plans):
        out = lax.dynamic_update_slice_in_dim(out, acc, base + ((p + 1) % n) * chunk, axis=1)
    curs = accs
    for k in range(n - 1):
        curs = [lax.ppermute(cur, axis, plan[2]) for cur, plan in zip(curs, plans)]
        if k == n // 2:
            lead, hold = lax.optimization_barrier((curs[0], hold))
            curs = [lead] + curs[1:]
        for cur, (base, p, _) in zip(curs, plans):
            out = lax.dynamic_update_slice_in_dim(out, cur, base + ((p - k) % n) * chunk, axis=1)
    return out, hold


def shards(inputs, grad_out, weights):
    planes, ny, nz, fshare = grad_out.shape
    cin = weights.shape[3]
    voxels = planes * ny * nz
    scale = 1.0 / math.sqrt(voxels * lax.axis_size("space"))
    grad_rimmed = extended(grad_out, (("space", 0),), 1)
    grad_padded = jnp.pad(grad_rimmed, ((0, 0), (1, 1), (1, 1), (0, 0)))
    gathered = lax.all_gather(inputs, "filt", axis=3, tiled=True)
    width = gathered.shape[3]
    data_term = jnp.zeros((voxels, cin), jnp.float32)
    for a in (1, 0, 2):
        moved_list = []
        for data_b in range(3):
            for data_c in range(3):
                moved_list.append(
                    grad_padded[
                        2 - a : 2 - a + planes,
                        2 - data_b : 2 - data_b + ny,
                        2 - data_c : 2 - data_c + nz,
                        :,
                    ].reshape(voxels, fshare)
                )
        stacked = jnp.stack(moved_list, axis=1).reshape(voxels, 3, 3, fshare)
        data_term = data_term + lax.dot_general(
            stacked,
            weights[a],
            (((1, 2, 3), (0, 1, 3)), ((), ())),
            preferred_element_type=jnp.float32,
        )
    fsplit = lax.axis_size("filt") == 4
    own_half = None
    if fsplit:
        f = lax.axis_index("filt")
        partner = lax.ppermute(inputs, "filt", [(i, i ^ 1) for i in range(4)])
        own_half = jnp.where(
            f % 2 == 0,
            jnp.concatenate([inputs, partner], axis=3),
            jnp.concatenate([partner, inputs], axis=3),
        )
    data_term, gathered, own_half = lax.optimization_barrier((data_term, gathered, own_half))
    grad_inputs = lax.psum_scatter(
        data_term.reshape(planes, ny, nz, cin), "filt", scatter_dimension=3, tiled=True
    ).astype(jnp.bfloat16)
    in_t = gathered.reshape(voxels, width)
    if fsplit:
        f = lax.axis_index("filt")
        first = weight_taps(own_half.reshape(voxels, width // 2), grad_padded, 0, 1)
        first, in_t = lax.optimization_barrier((first, in_t))
        other_half = lax.dynamic_slice_in_dim(in_t, (1 - f // 2) * (width // 2), width // 2, axis=1)
        second = weight_taps(other_half, grad_padded, 0, 1)
        bases = [(f // 2) * (width // 2), (1 - f // 2) * (width // 2)]
    else:
        first = weight_taps(in_t, grad_padded, 0, 2)
        second = weight_taps(in_t, grad_padded, 1, 2)
        bases = [0, width // 2]
    summed, grad_inputs = ring_sum([first, second], bases, "space", scale, grad_inputs)
    weight_grad = summed.reshape(3, 3, 3, width, fshare)
    return (grad_inputs, weight_grad)


def solution(mesh):
    placed = (
        P("space", None, None, "filt"),
        P("space", None, None, "filt"),
        P(None, None, None, None, "filt"),
    )
    return jax.shard_map(
        shards,
        mesh=mesh,
        in_specs=placed,
        out_specs=(P("space", None, None, "filt"), P(None, None, None, None, "filt")),
        check_vma=False,
    )
```
